1024 devices in a mesh: lat: 16 (over x, core), lon: 64 (over y, z).
Axes of the slice: x: 8, y: 8, z: 8, core: 2. Of those that a mesh axis runs over, the one named last changes fastest.
Arguments:
- grid_field: bfloat16 [8, 2, 1024, 4160], P(None, None, 'lat', 'lon'), may hold values from -6 to 6
- row_shift: int32 [2, 1024, 4160], P(None, 'lat', 'lon'), may hold values from -1 to 1
- col_shift: int32 [2, 1024, 4160], P(None, 'lat', 'lon'), may hold values from -4 to 4
- lon_weight: bfloat16 [2, 1024, 4160], P(None, 'lat', 'lon'), may hold values from 0 to 1
- pair_of_slot: int32 [640], replicated, may hold values from 0 to 639, each once
- legendre: bfloat16 [1024, 640, 1281], P('lat', 'lon'), may hold values from -0.125 to 0.125
- helm_coeff: float32 [8], replicated, may hold values from 1e-07 to 1e-05
Outputs:
- spectral_solution: float32 [640, 2, 8, 1281], P('lon')
- fourier_rows: bfloat16 [640, 2, 2, 2, 8, 1024], P('lon', None, None, None, None, 'lat')
The draws below stay inside these ranges and needn't reach their ends.
Inputs may be any that keep to these rules, and one draw needn't show every extreme that they name: `pair_of_slot`: each of the 640 pair numbers stands in exactly one slot.
All inputs are finite; a program needn't handle non-finite values.
Results may differ from the reference program's by a relative error of at most 0.0066.
Values may be sent and summed in bfloat16 or wider, within the bound.
No kernel may reach another device: no remote copies, remote signals or barrier semaphores. Data moves between devices by JAX's collectives and lax.ppermute only.
A program may use at most 64 MiB of HBM per device.

```python
import math
import jax
import jax.numpy as jnp
from jax import lax

TRUNC = 1279
NHALF = 1024
FL = 8
H = 1
S = 4
NLAT = 2048
NLONP = 4160
PAIRS = 640
NPAIR = 1281


def plant(drawn, own_key, least, high):
    extent = drawn.shape
    index_at = [jax.random.randint(jax.random.fold_in(own_key, axis), (), 0, extent[axis]) for axis in range(len(extent))]
    drawn = drawn.at[tuple(index_at)].set(least)
    longest = extent.index(max(extent))
    index_at[longest] = (index_at[longest] + 1) % extent[longest]
    return drawn.at[tuple(index_at)].set(high)


def levels(key, shape, pieces, low, high):
    factor_of, own = 1.0, jax.random.fold_in(key, 6)
    for axis_at, parts in pieces:
        draws = jnp.exp(jax.random.uniform(jax.random.fold_in(own, axis_at), (parts,), jnp.float32, low / len(pieces), high / len(pieces)))
        factor_of = factor_of * jnp.repeat(draws, shape[axis_at] // parts).reshape([-1 if axis == axis_at else 1 for axis in range(len(shape))])
    return factor_of


def centred(own_key, shape, scale, most, cuts=(), kind=jnp.bfloat16):
    array = jax.random.normal(own_key, shape, jnp.float32) * scale
    if len(cuts) > 0:
        array = levels(own_key, shape, cuts, -0.22, 0.18) * array
    return jnp.clip(array, min=-most, max=most).astype(kind)


def setup_inputs(seed: int = 0) -> dict:
    seeds = jax.random.split(jax.random.key(seed), 8)
    return {
        "grid_field": centred(seeds[0], (FL, 2, NHALF, NLONP), 1.0, 6.0, ((2, 16), (3, 64))),
        "row_shift": plant(jax.random.randint(seeds[1], (2, NHALF, NLONP), 0 - H, H + 1), jax.random.fold_in(seeds[1], 1), 0 - H, H).astype(jnp.int32),
        "col_shift": plant(jax.random.randint(seeds[2], (2, NHALF, NLONP), 0 - S, S + 1), jax.random.fold_in(seeds[2], 1), 0 - S, S).astype(jnp.int32),
        "lon_weight": jnp.clip(1.0 * jax.random.uniform(seeds[3], (2, NHALF, NLONP), jnp.float32) ** levels(seeds[3], (2, NHALF, NLONP), ((1, 16), (2, 64)), -0.2, 0.2), 0.0, 1.0).astype(jnp.bfloat16),
        "pair_of_slot": jax.random.permutation(seeds[4], PAIRS).astype(jnp.int32),
        "legendre": centred(seeds[5], (NHALF, PAIRS, NPAIR), NLAT ** -0.5, 0.125, ((0, 16), (1, 64))),
        "helm_coeff": jnp.clip(jnp.exp(jax.random.uniform(seeds[6], (FL,), jnp.float32, math.log(1.0000000116860974e-07), math.log(9.999999747378752e-06))), 1.0000000116860974e-07, 9.999999747378752e-06),
    }


def depart_values(extended, low_rows, first_row, col_core, col_ext, row_shift, col_shift, lon_weight):
    row_count = row_shift.shape[1]
    col_count = row_shift.shape[2]
    height = extended.shape[2]
    ext_width = extended.shape[3]
    lat_index = first_row + jnp.arange(row_count, dtype=jnp.int32)[:, None]
    lon_index = col_core + jnp.arange(col_count, dtype=jnp.int32)[None, :]
    length = 20 + 4 * lat_index
    target = jnp.maximum(lat_index + row_shift, 0)
    mirror = jnp.where(target > NHALF - 1, 2 * NHALF - 1 - target, target)
    length_dep = 20 + 4 * mirror
    shifted = jnp.clip(lon_index + col_shift, 0, length - 1)
    column = jnp.minimum(shifted * length_dep // length, length_dep - 2)
    hemisphere = jnp.arange(2, dtype=jnp.int32)[:, None, None]
    flat_index = (hemisphere * height + (target - first_row + low_rows)) * ext_width + (column - col_ext)
    flat_field = extended.reshape(extended.shape[0], -1)
    left_value = flat_field[:, flat_index].astype(jnp.float32)
    right_value = flat_field[:, flat_index + 1].astype(jnp.float32)
    blend = lon_weight.astype(jnp.float32)
    blended = (1.0 - blend) * left_value + blend * right_value
    return jnp.where(lon_index < length, blended, 0.0).astype(jnp.bfloat16)

def one_row(row_item):
    row_data, lat_index = row_item
    length = 20 + 4 * lat_index
    quarter_len = length // 4
    slots = jnp.arange(NLONP // 4, dtype=jnp.int32)[:, None]
    orders = jnp.arange(TRUNC + 1, dtype=jnp.int32)[None, :]
    phase_idx = orders * slots % quarter_len
    angles = phase_idx.astype(jnp.float32) * (2.0 * math.pi) / quarter_len.astype(jnp.float32)
    usable = (2 * orders < length) & (slots < quarter_len)
    cosine = jnp.where(usable, jnp.cos(angles), 0.0)
    minus_sine = jnp.where(usable, -jnp.sin(angles), 0.0)
    factors = jnp.stack([cosine, minus_sine], axis=-1).astype(jnp.bfloat16)
    quarters = row_data.reshape(row_data.shape[0], 2, -1, 4)
    inner = jnp.einsum('amr,fhab->mrfhb', factors.astype(jnp.float32), quarters.astype(jnp.float32), precision=lax.Precision.HIGHEST)
    offsets = jnp.arange(4, dtype=jnp.int32)[None, :]
    twist_idx = jnp.arange(TRUNC + 1, dtype=jnp.int32)[:, None] * offsets % length
    twist = twist_idx.astype(jnp.float32) * (2.0 * math.pi) / length.astype(jnp.float32)
    twist_cos = jnp.cos(twist)[:, None, None, :]
    twist_sin = jnp.sin(twist)[:, None, None, :]
    real_part = lax.optimization_barrier(jnp.sum(inner[:, 0] * twist_cos + inner[:, 1] * twist_sin, axis=-1))
    imag_part = lax.optimization_barrier(jnp.sum(inner[:, 1] * twist_cos - inner[:, 0] * twist_sin, axis=-1))
    spectrum = jnp.stack([real_part, imag_part], axis=1)
    norm_scale = 1.0 / jnp.sqrt(length.astype(jnp.float32))
    return (spectrum * norm_scale).astype(jnp.bfloat16)

def column_terms(pair_ids):
    columns = jnp.arange(NPAIR, dtype=jnp.int32)[None, :]
    partner = (TRUNC - pair_ids)[:, None]
    second_half = columns > partner
    degree = jnp.where(second_half, columns - 1, pair_ids[:, None] + columns)
    offset = jnp.where(second_half, columns - 1 - partner, columns)
    parity = (1 - 2 * (offset % 2)).astype(jnp.float32)
    return (second_half, degree, parity)

def analyse(legend, spectra, pair_ids):
    products = jnp.einsum('ksc,ksq->sqc', legend.astype(jnp.float32), spectra.astype(jnp.float32), precision=lax.Precision.HIGHEST)
    second_half, degree, parity = column_terms(pair_ids)
    products = products.reshape(products.shape[0], 2, 2, -1, 2, NPAIR)
    chosen = jnp.where(second_half[:, None, None, None, :], products[:, 1], products[:, 0])
    return chosen[:, :, :, 0] + parity[:, None, None, :] * chosen[:, :, :, 1]

def helmholtz_solve(spectral_total, pair_ids, helm_coeff):
    second_half, degree, parity = column_terms(pair_ids)
    growth = (degree * (degree + 1)).astype(jnp.float32)
    return spectral_total / (1.0 + helm_coeff[None, None, :, None] * growth[:, None, None, :])

def synthesise(legend, solved, pair_ids):
    second_half, degree, parity = column_terms(pair_ids)
    rounded = solved.astype(jnp.bfloat16)
    lower_mask = jnp.where(second_half, 0.0, 1.0)
    upper_mask = jnp.where(second_half, 1.0, 0.0)
    selector = jnp.stack([lower_mask, upper_mask], axis=1)
    sign_rows = jnp.stack([jnp.ones_like(parity), parity], axis=1)
    weights = (selector[:, :, None, :] * sign_rows[:, None, :, :]).astype(jnp.bfloat16)
    spread = weights[:, :, :, None, None, :] * rounded[:, None, None, :, :, :]
    out_shape = spread.shape[:5]
    spread = spread.reshape(spread.shape[0], -1, NPAIR)
    rows_out = jnp.einsum('ksc,sqc->sqk', legend.astype(jnp.float32), spread.astype(jnp.float32), precision=lax.Precision.HIGHEST)
    rows_out = (4.0 * rows_out).astype(jnp.bfloat16)
    return rows_out.reshape(out_shape + (legend.shape[0],))

def reference(grid_field, row_shift, col_shift, lon_weight, pair_of_slot, legendre, helm_coeff):
    mirrored = grid_field[:, ::-1, NHALF - H:, :][:, :, ::-1, :]
    extended = jnp.concatenate([grid_field, mirrored], axis=2)
    advected = depart_values(extended, 0, 0, 0, 0, row_shift, col_shift, lon_weight)
    per_row = jnp.moveaxis(advected, 2, 0)
    lat_rows = jnp.arange(NHALF, dtype=jnp.int32)
    fourier = lax.map(one_row, (per_row, lat_rows))

    def one_slot(slot_index):
        pair_ids = lax.dynamic_slice_in_dim(pair_of_slot, slot_index.astype(jnp.int32), 1)
        leg_table = lax.dynamic_slice_in_dim(legendre, slot_index.astype(jnp.int32), 1, 1)
        orders = jnp.concatenate([pair_ids, TRUNC - pair_ids]).astype(jnp.int32)
        picked = jnp.take(fourier, orders, axis=1)
        spectra = picked.reshape(NHALF, 1, -1)
        partial_sum = analyse(leg_table, spectra, pair_ids)
        solved = helmholtz_solve(partial_sum, pair_ids, helm_coeff)
        return (solved[0], synthesise(leg_table, solved, pair_ids)[0])
    spectral_solution, fourier_rows = lax.map(one_slot, jnp.arange(PAIRS, dtype=jnp.int32))
    return (spectral_solution, fourier_rows)
```

```python
import math

import jax
import jax.numpy as jnp
from jax import lax
from jax.sharding import PartitionSpec as P

TRUNC = 1279
H = 1
PAIRS = 640
NPAIR = 1281
WL = 10


def extended_2(value, sides, width):
    for axis, dim in sides:
        peers, length = (lax.axis_size(axis), value.shape[dim])
        up = [(i, (i + 1) % peers) for i in range(peers - 1)]
        down = [(j, i) for i, j in up]
        last = lax.slice_in_dim(value, length - width, length, axis=dim)
        initial = lax.slice_in_dim(value, 0, width, axis=dim)
        before = lax.ppermute(last, axis, up)
        after = lax.ppermute(initial, axis, down)
        value = jnp.concatenate([before, value, after], axis=dim)
    return value


def shortened(value):

    def short(part):
        return part.astype(jnp.bfloat16) if part.dtype == jnp.float32 else part

    return jax.tree.map(short, value)


def depart_values(
    extended, half_rows, low_rows, first_row, col_core, col_ext, row_shift, col_shift, lon_weight
):
    row_count = row_shift.shape[1]
    col_count = row_shift.shape[2]
    height = extended.shape[2]
    ext_width = extended.shape[3]
    lat_index = first_row + jnp.arange(row_count, dtype=jnp.int32)[:, None]
    lon_index = col_core + jnp.arange(col_count, dtype=jnp.int32)[None, :]
    length = 20 + 4 * lat_index
    target = jnp.maximum(lat_index + row_shift, 0)
    mirror = jnp.where(target > half_rows - 1, 2 * half_rows - 1 - target, target)
    length_dep = 20 + 4 * mirror
    shifted = jnp.clip(lon_index + col_shift, 0, length - 1)
    column = jnp.minimum(shifted * length_dep // length, length_dep - 2)
    hemisphere = jnp.arange(2, dtype=jnp.int32)[:, None, None]
    flat_index = (hemisphere * height + (target - first_row + low_rows)) * ext_width + (
        column - col_ext
    )
    flat_field = extended.reshape(extended.shape[0], -1)
    left_value = flat_field[:, flat_index].astype(jnp.float32)
    right_value = flat_field[:, flat_index + 1].astype(jnp.float32)
    blend = lon_weight.astype(jnp.float32)
    blended = (1.0 - blend) * left_value + blend * right_value
    return jnp.where(lon_index < length, blended, 0.0).astype(jnp.bfloat16)


def phase_table(orders, steps, quarter_len):
    phase_idx = orders[None] * steps[:, None, None] % quarter_len
    angles = phase_idx.astype(jnp.float32) * (2.0 * math.pi) / quarter_len.astype(jnp.float32)
    return jnp.cos(angles), jnp.sin(angles)


def row_spectrum(row_data, lat_index, pair_of_slot):
    length = 20 + 4 * lat_index
    quarter_len = length // 4
    quarters = row_data.reshape(row_data.shape[0], 2, -1, 4)
    slot_count = quarters.shape[2]
    inner_n = 32
    outer_n = -(-slot_count // inner_n)
    offsets = jnp.arange(4, dtype=jnp.int32)[None, None, :]
    norm_scale = 1.0 / jnp.sqrt(length.astype(jnp.float32))
    pair_orders = jnp.stack([pair_of_slot, TRUNC - pair_of_slot], axis=1)
    outer_cos, outer_sin = phase_table(
        pair_orders, jnp.arange(outer_n, dtype=jnp.int32) * inner_n, quarter_len
    )
    inner_cos, inner_sin = phase_table(pair_orders, jnp.arange(inner_n, dtype=jnp.int32), quarter_len)
    cosine = outer_cos[:, None] * inner_cos[None] - outer_sin[:, None] * inner_sin[None]
    minus_sine = -(outer_sin[:, None] * inner_cos[None] + outer_cos[:, None] * inner_sin[None])
    cosine = cosine.reshape((outer_n * inner_n,) + cosine.shape[2:])[:slot_count]
    minus_sine = minus_sine.reshape((outer_n * inner_n,) + minus_sine.shape[2:])[:slot_count]
    slots = jnp.arange(slot_count, dtype=jnp.int32)[:, None, None]
    usable = (2 * pair_orders[None] < length) & (slots < quarter_len)
    factors = jnp.stack(
        [jnp.where(usable, cosine, 0.0), jnp.where(usable, minus_sine, 0.0)], axis=-1
    ).astype(jnp.bfloat16)
    inner = jnp.einsum("aser,fhab->serfhb", factors, quarters, preferred_element_type=jnp.float32)
    twist_idx = pair_orders[:, :, None] * offsets % length
    twist = twist_idx.astype(jnp.float32) * (2.0 * math.pi) / length.astype(jnp.float32)
    twist_cos = jnp.cos(twist)[:, :, None, None, :]
    twist_sin = jnp.sin(twist)[:, :, None, None, :]
    real_part = jnp.sum(inner[:, :, 0] * twist_cos + inner[:, :, 1] * twist_sin, axis=-1)
    imag_part = jnp.sum(inner[:, :, 1] * twist_cos - inner[:, :, 0] * twist_sin, axis=-1)
    spectrum = jnp.stack([real_part, imag_part], axis=2)
    return (spectrum * norm_scale).astype(jnp.bfloat16).reshape(PAIRS, -1)


def lat_sum(value):
    peers = lax.axis_size("lat")
    count = value.size
    pad = (-count) % (peers * 1024)
    flat = jnp.pad(value.reshape(-1), (0, pad)).reshape(peers, -1, 1024)
    pieces = lax.all_to_all(flat, "lat", 0, 0, tiled=True)
    reduced = jnp.sum(pieces, axis=0, keepdims=True)
    whole = lax.all_gather(reduced, "lat", axis=0, tiled=True)
    return whole.reshape(-1)[:count].reshape(value.shape)


def column_terms(pair_ids):
    columns = jnp.arange(NPAIR, dtype=jnp.int32)[None, :]
    partner = (TRUNC - pair_ids)[:, None]
    second_half = columns > partner
    degree = jnp.where(second_half, columns - 1, pair_ids[:, None] + columns)
    offset = jnp.where(second_half, columns - 1 - partner, columns)
    parity = (1 - 2 * (offset % 2)).astype(jnp.float32)
    return (second_half, degree, parity)


def analyse(legend, spectra, pair_ids):
    products = jnp.einsum("ksc,ksq->sqc", legend, spectra, preferred_element_type=jnp.float32)
    second_half, degree, parity = column_terms(pair_ids)
    products = products.reshape(products.shape[0], 2, 2, -1, 2, NPAIR)
    chosen = jnp.where(second_half[:, None, None, None, :], products[:, 1], products[:, 0])
    return chosen[:, :, :, 0] + parity[:, None, None, :] * chosen[:, :, :, 1]


def helmholtz_solve(spectral_total, pair_ids, helm_coeff):
    second_half, degree, parity = column_terms(pair_ids)
    growth = (degree * (degree + 1)).astype(jnp.float32)
    return spectral_total / (1.0 + helm_coeff[None, None, :, None] * growth[:, None, None, :])


def synthesise(legend, solved, pair_ids):
    second_half, degree, parity = column_terms(pair_ids)
    rounded = solved.astype(jnp.bfloat16)
    lower_mask = jnp.where(second_half, 0.0, 1.0)
    upper_mask = jnp.where(second_half, 1.0, 0.0)
    selector = jnp.stack([lower_mask, upper_mask], axis=1)
    sign_rows = jnp.stack([jnp.ones_like(parity), parity], axis=1)
    weights = (selector[:, :, None, :] * sign_rows[:, None, :, :]).astype(jnp.bfloat16)
    spread = weights[:, :, :, None, None, :] * rounded[:, None, None, :, :, :]
    out_shape = spread.shape[:5]
    spread = spread.reshape(spread.shape[0], -1, NPAIR)
    rows_out = jnp.einsum("ksc,sqc->sqk", legend, spread, preferred_element_type=jnp.float32)
    rows_out = (4.0 * rows_out).astype(jnp.bfloat16)
    return rows_out.reshape(out_shape + (legend.shape[0],))


def on_device(grid_field, row_shift, col_shift, lon_weight, pair_of_slot, legendre, helm_coeff):
    lat_pos = lax.axis_index("lat")
    lon_pos = lax.axis_index("lon")
    lat_count = lax.axis_size("lat")
    lon_count = lax.axis_size("lon")
    band_rows = grid_field.shape[2]
    sector_cols = grid_field.shape[3]
    half_rows = band_rows * lat_count
    row_count = band_rows // lon_count
    first_row = lat_pos * band_rows + lon_pos * row_count
    widened = extended_2(grid_field, (("lon", 3),), WL)
    extended = extended_2(widened, (("lat", 2),), H)
    mirrored = widened[:, ::-1, band_rows - H :, :][:, :, ::-1, :]
    at_equator = lat_pos == lat_count - 1
    upper_rows = jnp.where(at_equator, mirrored, extended[:, :, band_rows + H :, :])
    extended = jnp.concatenate([extended[:, :, : band_rows + H, :], upper_rows], axis=2)
    advected = depart_values(
        extended,
        half_rows,
        H,
        lat_pos * band_rows,
        lon_pos * sector_cols,
        lon_pos * sector_cols - WL,
        row_shift,
        col_shift,
        lon_weight,
    )
    row_data = lax.all_to_all(advected, "lon", split_axis=2, concat_axis=3, tiled=True)
    lat_rows = first_row + jnp.arange(row_count, dtype=jnp.int32)
    per_row = jnp.moveaxis(row_data, 2, 0)

    def spectrum_of_row(row_item):
        return row_spectrum(row_item[0], row_item[1], pair_of_slot)

    spectra = lax.map(spectrum_of_row, (per_row, lat_rows))
    gathered = jax.tree.map(
        lambda part, own: part.astype(own.dtype),
        lax.all_to_all(shortened(spectra), "lon", split_axis=1, concat_axis=0, tiled=True),
        spectra,
    )
    slot_count = legendre.shape[1]
    pair_ids = lax.dynamic_slice_in_dim(pair_of_slot, lon_pos * slot_count, slot_count)
    partial_sum = analyse(legendre, gathered, pair_ids)
    spectral_total = lat_sum(partial_sum)
    spectral_solution = helmholtz_solve(spectral_total, pair_ids, helm_coeff)
    fourier_rows = synthesise(legendre, spectral_solution, pair_ids)
    return (spectral_solution, fourier_rows)


def solution(mesh):
    return jax.shard_map(
        on_device,
        mesh=mesh,
        in_specs=(
            P(None, None, "lat", "lon"),
            P(None, "lat", "lon"),
            P(None, "lat", "lon"),
            P(None, "lat", "lon"),
            P(),
            P("lat", "lon", None),
            P(),
        ),
        out_specs=(P("lon", None, None, None), P("lon", None, None, None, None, "lat")),
        check_vma=False,
    )
```

```python
import math

import jax
import jax.numpy as jnp
from jax import lax
from jax.sharding import PartitionSpec as P

TRUNC = 1279
H = 1
PAIRS = 640
NPAIR = 1281
WL = 10


def extended_2(value, sides, width):
    for axis, dim in sides:
        peers, length = (lax.axis_size(axis), value.shape[dim])
        up = [(i, (i + 1) % peers) for i in range(peers - 1)]
        down = [(j, i) for i, j in up]
        last = lax.slice_in_dim(value, length - width, length, axis=dim)
        initial = lax.slice_in_dim(value, 0, width, axis=dim)
        before = lax.ppermute(last, axis, up)
        after = lax.ppermute(initial, axis, down)
        value = jnp.concatenate([before, value, after], axis=dim)
    return value


def shortened(value):

    def short(part):
        return part.astype(jnp.bfloat16) if part.dtype == jnp.float32 else part

    return jax.tree.map(short, value)


def depart_values(
    extended, half_rows, low_rows, first_row, col_core, col_ext, row_shift, col_shift, lon_weight
):
    row_count = row_shift.shape[1]
    col_count = row_shift.shape[2]
    height = extended.shape[2]
    ext_width = extended.shape[3]
    lat_index = first_row + jnp.arange(row_count, dtype=jnp.int32)[:, None]
    lon_index = col_core + jnp.arange(col_count, dtype=jnp.int32)[None, :]
    length = 20 + 4 * lat_index
    target = jnp.maximum(lat_index + row_shift, 0)
    mirror = jnp.where(target > half_rows - 1, 2 * half_rows - 1 - target, target)
    length_dep = 20 + 4 * mirror
    shifted = jnp.clip(lon_index + col_shift, 0, length - 1)
    column = jnp.minimum(shifted * length_dep // length, length_dep - 2)
    row_off = target - first_row + low_rows - (lat_index - first_row)
    col_off = column - col_ext - (lon_index - col_core)
    left_value = jnp.zeros(extended.shape[:2] + row_shift.shape[1:], extended.dtype)
    right_value = left_value
    for dr in range(height - row_count + 1):
        row_hit = row_off == dr
        for dc in range(1, ext_width - col_count - 1):
            window = extended[:, :, dr : dr + row_count, dc : dc + col_count]
            left_value = jnp.where(row_hit & (col_off == dc), window, left_value)
            right_value = jnp.where(row_hit & (col_off + 1 == dc), window, right_value)
    left_value = left_value.astype(jnp.float32)
    right_value = right_value.astype(jnp.float32)
    blend = lon_weight.astype(jnp.float32)
    blended = (1.0 - blend) * left_value + blend * right_value
    return jnp.where(lon_index < length, blended, 0.0).astype(jnp.bfloat16)


def phase_table(orders, steps, quarter_len):
    phase_idx = orders[None] * steps[:, None, None] % quarter_len
    angles = phase_idx.astype(jnp.float32) * (2.0 * math.pi) / quarter_len.astype(jnp.float32)
    return jnp.cos(angles), jnp.sin(angles)


def row_spectrum(row_data, lat_index, pair_of_slot):
    length = 20 + 4 * lat_index
    quarter_len = length // 4
    quarters = row_data.reshape(row_data.shape[0], 2, -1, 4)
    slot_count = quarters.shape[2]
    inner_n = 32
    outer_n = -(-slot_count // inner_n)
    offsets = jnp.arange(4, dtype=jnp.int32)[None, None, :]
    norm_scale = 1.0 / jnp.sqrt(length.astype(jnp.float32))
    pair_orders = jnp.stack([pair_of_slot, TRUNC - pair_of_slot], axis=1)
    outer_cos, outer_sin = phase_table(
        pair_orders, jnp.arange(outer_n, dtype=jnp.int32) * inner_n, quarter_len
    )
    inner_cos, inner_sin = phase_table(pair_orders, jnp.arange(inner_n, dtype=jnp.int32), quarter_len)
    cosine = outer_cos[:, None] * inner_cos[None] - outer_sin[:, None] * inner_sin[None]
    minus_sine = -(outer_sin[:, None] * inner_cos[None] + outer_cos[:, None] * inner_sin[None])
    cosine = cosine.reshape((outer_n * inner_n,) + cosine.shape[2:])[:slot_count]
    minus_sine = minus_sine.reshape((outer_n * inner_n,) + minus_sine.shape[2:])[:slot_count]
    slots = jnp.arange(slot_count, dtype=jnp.int32)[:, None, None]
    usable = (2 * pair_orders[None] < length) & (slots < quarter_len)
    factors = jnp.stack(
        [jnp.where(usable, cosine, 0.0), jnp.where(usable, minus_sine, 0.0)], axis=-1
    ).astype(jnp.bfloat16)
    inner = jnp.einsum("aser,fhab->serfhb", factors, quarters, preferred_element_type=jnp.float32)
    twist_idx = pair_orders[:, :, None] * offsets % length
    twist = twist_idx.astype(jnp.float32) * (2.0 * math.pi) / length.astype(jnp.float32)
    twist_cos = jnp.cos(twist)[:, :, None, None, :]
    twist_sin = jnp.sin(twist)[:, :, None, None, :]
    real_part = jnp.sum(inner[:, :, 0] * twist_cos + inner[:, :, 1] * twist_sin, axis=-1)
    imag_part = jnp.sum(inner[:, :, 1] * twist_cos - inner[:, :, 0] * twist_sin, axis=-1)
    spectrum = jnp.stack([real_part, imag_part], axis=2)
    return (spectrum * norm_scale).astype(jnp.bfloat16).reshape(PAIRS, -1)


def lat_sum(value):
    peers = lax.axis_size("lat")
    count = value.size
    pad = (-count) % (peers * 1024)
    flat = jnp.pad(value.reshape(-1), (0, pad)).reshape(peers, -1, 1024)
    pieces = lax.all_to_all(flat, "lat", 0, 0, tiled=True)
    reduced = jnp.sum(pieces, axis=0, keepdims=True)
    whole = lax.all_gather(reduced, "lat", axis=0, tiled=True)
    return whole.reshape(-1)[:count].reshape(value.shape)


def column_terms(pair_ids):
    columns = jnp.arange(NPAIR, dtype=jnp.int32)[None, :]
    partner = (TRUNC - pair_ids)[:, None]
    second_half = columns > partner
    degree = jnp.where(second_half, columns - 1, pair_ids[:, None] + columns)
    offset = jnp.where(second_half, columns - 1 - partner, columns)
    parity = (1 - 2 * (offset % 2)).astype(jnp.float32)
    return (second_half, degree, parity)


def analyse(legend, spectra, pair_ids):
    products = jnp.einsum("ksc,ksq->sqc", legend, spectra, preferred_element_type=jnp.float32)
    second_half, degree, parity = column_terms(pair_ids)
    products = products.reshape(products.shape[0], 2, 2, -1, 2, NPAIR)
    chosen = jnp.where(second_half[:, None, None, None, :], products[:, 1], products[:, 0])
    return chosen[:, :, :, 0] + parity[:, None, None, :] * chosen[:, :, :, 1]


def helmholtz_solve(spectral_total, pair_ids, helm_coeff):
    second_half, degree, parity = column_terms(pair_ids)
    growth = (degree * (degree + 1)).astype(jnp.float32)
    return spectral_total / (1.0 + helm_coeff[None, None, :, None] * growth[:, None, None, :])


def synthesise(legend, solved, pair_ids):
    second_half, degree, parity = column_terms(pair_ids)
    rounded = solved.astype(jnp.bfloat16)
    lower_mask = jnp.where(second_half, 0.0, 1.0)
    upper_mask = jnp.where(second_half, 1.0, 0.0)
    selector = jnp.stack([lower_mask, upper_mask], axis=1)
    sign_rows = jnp.stack([jnp.ones_like(parity), parity], axis=1)
    weights = (selector[:, :, None, :] * sign_rows[:, None, :, :]).astype(jnp.bfloat16)
    spread = weights[:, :, :, None, None, :] * rounded[:, None, None, :, :, :]
    out_shape = spread.shape[:5]
    spread = spread.reshape(spread.shape[0], -1, NPAIR)
    rows_out = jnp.einsum("ksc,sqc->sqk", legend, spread, preferred_element_type=jnp.float32)
    rows_out = (4.0 * rows_out).astype(jnp.bfloat16)
    return rows_out.reshape(out_shape + (legend.shape[0],))


def on_device(grid_field, row_shift, col_shift, lon_weight, pair_of_slot, legendre, helm_coeff):
    lat_pos = lax.axis_index("lat")
    lon_pos = lax.axis_index("lon")
    lat_count = lax.axis_size("lat")
    lon_count = lax.axis_size("lon")
    band_rows = grid_field.shape[2]
    sector_cols = grid_field.shape[3]
    half_rows = band_rows * lat_count
    row_count = band_rows // lon_count
    first_row = lat_pos * band_rows + lon_pos * row_count
    widened = extended_2(grid_field, (("lon", 3),), WL)
    extended = extended_2(widened, (("lat", 2),), H)
    mirrored = widened[:, ::-1, band_rows - H :, :][:, :, ::-1, :]
    at_equator = lat_pos == lat_count - 1
    upper_rows = jnp.where(at_equator, mirrored, extended[:, :, band_rows + H :, :])
    extended = jnp.concatenate([extended[:, :, : band_rows + H, :], upper_rows], axis=2)
    advected = depart_values(
        extended,
        half_rows,
        H,
        lat_pos * band_rows,
        lon_pos * sector_cols,
        lon_pos * sector_cols - WL,
        row_shift,
        col_shift,
        lon_weight,
    )
    row_data = lax.all_to_all(advected, "lon", split_axis=2, concat_axis=3, tiled=True)
    lat_rows = first_row + jnp.arange(row_count, dtype=jnp.int32)
    per_row = jnp.moveaxis(row_data, 2, 0)

    def spectrum_of_row(row_item):
        return row_spectrum(row_item[0], row_item[1], pair_of_slot)

    spectra = lax.map(spectrum_of_row, (per_row, lat_rows))
    gathered = jax.tree.map(
        lambda part, own: part.astype(own.dtype),
        lax.all_to_all(shortened(spectra), "lon", split_axis=1, concat_axis=0, tiled=True),
        spectra,
    )
    slot_count = legendre.shape[1]
    pair_ids = lax.dynamic_slice_in_dim(pair_of_slot, lon_pos * slot_count, slot_count)
    partial_sum = analyse(legendre, gathered, pair_ids)
    spectral_total = lat_sum(partial_sum)
    spectral_solution = helmholtz_solve(spectral_total, pair_ids, helm_coeff)
    fourier_rows = synthesise(legendre, spectral_solution, pair_ids)
    return (spectral_solution, fourier_rows)


def solution(mesh):
    return jax.shard_map(
        on_device,
        mesh=mesh,
        in_specs=(
            P(None, None, "lat", "lon"),
            P(None, "lat", "lon"),
            P(None, "lat", "lon"),
            P(None, "lat", "lon"),
            P(),
            P("lat", "lon", None),
            P(),
        ),
        out_specs=(P("lon", None, None, None), P("lon", None, None, None, None, "lat")),
        check_vma=False,
    )
```

```python
import math

import jax
import jax.numpy as jnp
from jax import lax
from jax.experimental import pallas as pl
from jax.sharding import PartitionSpec as P

TRUNC = 1279
H = 1
PAIRS = 640
NPAIR = 1281
WL = 10


def extended_2(value, sides, width):
    for axis, dim in sides:
        peers, length = (lax.axis_size(axis), value.shape[dim])
        up = [(i, (i + 1) % peers) for i in range(peers - 1)]
        down = [(j, i) for i, j in up]
        last = lax.slice_in_dim(value, length - width, length, axis=dim)
        initial = lax.slice_in_dim(value, 0, width, axis=dim)
        before = lax.ppermute(last, axis, up)
        after = lax.ppermute(initial, axis, down)
        value = jnp.concatenate([before, value, after], axis=dim)
    return value


def shortened(value):

    def short(part):
        return part.astype(jnp.bfloat16) if part.dtype == jnp.float32 else part

    return jax.tree.map(short, value)


def depart_kernel(ext_ref, code_ref, weight_ref, out_ref):
    code = code_ref[...]
    rows, cols = code.shape[1], code.shape[2]
    left = jnp.zeros(code.shape, jnp.float32)
    right = left
    for dr in range(ext_ref.shape[2] - rows + 1):
        for dc in range(1, ext_ref.shape[3] - cols - 1):
            window = ext_ref[0, :, dr : dr + rows, dc : dc + cols]
            key = dr * 64 + dc
            left = jnp.where(code == key, window, left)
            right = jnp.where(code == key - 1, window, right)
    blend = weight_ref[...]
    out_ref[0] = (1.0 - blend) * left + blend * right


def depart_values(
    extended, half_rows, low_rows, first_row, col_core, col_ext, row_shift, col_shift, lon_weight
):
    row_count = row_shift.shape[1]
    col_count = row_shift.shape[2]
    height = extended.shape[2]
    ext_width = extended.shape[3]
    lat_index = first_row + jnp.arange(row_count, dtype=jnp.int32)[:, None]
    lon_index = col_core + jnp.arange(col_count, dtype=jnp.int32)[None, :]
    length = 20 + 4 * lat_index
    target = jnp.maximum(lat_index + row_shift, 0)
    mirror = jnp.where(target > half_rows - 1, 2 * half_rows - 1 - target, target)
    length_dep = 20 + 4 * mirror
    shifted = jnp.clip(lon_index + col_shift, 0, length - 1)
    column = jnp.minimum(shifted * length_dep // length, length_dep - 2)
    row_off = target - first_row + low_rows - (lat_index - first_row)
    col_off = column - col_ext - (lon_index - col_core)
    code = jnp.where(lon_index < length, row_off * 64 + col_off, -4096).astype(jnp.int32)
    field_count = extended.shape[0]
    blended = pl.pallas_call(
        depart_kernel,
        grid=(field_count,),
        in_specs=[
            pl.BlockSpec((1,) + extended.shape[1:], lambda f: (f, 0, 0, 0)),
            pl.BlockSpec(code.shape, lambda f: (0, 0, 0)),
            pl.BlockSpec(code.shape, lambda f: (0, 0, 0)),
        ],
        out_specs=pl.BlockSpec((1,) + code.shape, lambda f: (f, 0, 0, 0)),
        out_shape=jax.ShapeDtypeStruct((field_count,) + code.shape, jnp.float32),
    )(extended.astype(jnp.float32), code, lon_weight.astype(jnp.float32))
    return jnp.where(lon_index < length, blended, 0.0).astype(jnp.bfloat16)


def phase_table(orders, steps, quarter_len):
    phase_idx = orders[None] * steps[:, None, None] % quarter_len
    angles = phase_idx.astype(jnp.float32) * (2.0 * math.pi) / quarter_len.astype(jnp.float32)
    return jnp.cos(angles), jnp.sin(angles)


def row_spectrum(row_data, lat_index, pair_of_slot):
    length = 20 + 4 * lat_index
    quarter_len = length // 4
    quarters = row_data.reshape(row_data.shape[0], 2, -1, 4)
    slot_count = quarters.shape[2]
    inner_n = 32
    outer_n = -(-slot_count // inner_n)
    offsets = jnp.arange(4, dtype=jnp.int32)[None, None, :]
    norm_scale = 1.0 / jnp.sqrt(length.astype(jnp.float32))
    pair_orders = jnp.stack([pair_of_slot, TRUNC - pair_of_slot], axis=1)
    outer_cos, outer_sin = phase_table(
        pair_orders, jnp.arange(outer_n, dtype=jnp.int32) * inner_n, quarter_len
    )
    inner_cos, inner_sin = phase_table(pair_orders, jnp.arange(inner_n, dtype=jnp.int32), quarter_len)
    cosine = outer_cos[:, None] * inner_cos[None] - outer_sin[:, None] * inner_sin[None]
    minus_sine = -(outer_sin[:, None] * inner_cos[None] + outer_cos[:, None] * inner_sin[None])
    cosine = cosine.reshape((outer_n * inner_n,) + cosine.shape[2:])[:slot_count]
    minus_sine = minus_sine.reshape((outer_n * inner_n,) + minus_sine.shape[2:])[:slot_count]
    slots = jnp.arange(slot_count, dtype=jnp.int32)[:, None, None]
    usable = (2 * pair_orders[None] < length) & (slots < quarter_len)
    factors = jnp.stack(
        [jnp.where(usable, cosine, 0.0), jnp.where(usable, minus_sine, 0.0)], axis=-1
    ).astype(jnp.bfloat16)
    inner = jnp.einsum("aser,fhab->serfhb", factors, quarters, preferred_element_type=jnp.float32)
    twist_idx = pair_orders[:, :, None] * offsets % length
    twist = twist_idx.astype(jnp.float32) * (2.0 * math.pi) / length.astype(jnp.float32)
    twist_cos = jnp.cos(twist)[:, :, None, None, :]
    twist_sin = jnp.sin(twist)[:, :, None, None, :]
    real_part = jnp.sum(inner[:, :, 0] * twist_cos + inner[:, :, 1] * twist_sin, axis=-1)
    imag_part = jnp.sum(inner[:, :, 1] * twist_cos - inner[:, :, 0] * twist_sin, axis=-1)
    spectrum = jnp.stack([real_part, imag_part], axis=2)
    return (spectrum * norm_scale).astype(jnp.bfloat16).reshape(PAIRS, -1)


def lat_sum(value):
    peers = lax.axis_size("lat")
    count = value.size
    pad = (-count) % (peers * 1024)
    flat = jnp.pad(value.reshape(-1), (0, pad)).reshape(peers, -1, 1024)
    pieces = lax.all_to_all(flat, "lat", 0, 0, tiled=True)
    reduced = jnp.sum(pieces, axis=0, keepdims=True)
    whole = lax.all_gather(reduced, "lat", axis=0, tiled=True)
    return whole.reshape(-1)[:count].reshape(value.shape)


def column_terms(pair_ids):
    columns = jnp.arange(NPAIR, dtype=jnp.int32)[None, :]
    partner = (TRUNC - pair_ids)[:, None]
    second_half = columns > partner
    degree = jnp.where(second_half, columns - 1, pair_ids[:, None] + columns)
    offset = jnp.where(second_half, columns - 1 - partner, columns)
    parity = (1 - 2 * (offset % 2)).astype(jnp.float32)
    return (second_half, degree, parity)


def analyse(legend, spectra, pair_ids):
    products = jnp.einsum("ksc,ksq->sqc", legend, spectra, preferred_element_type=jnp.float32)
    second_half, degree, parity = column_terms(pair_ids)
    products = products.reshape(products.shape[0], 2, 2, -1, 2, NPAIR)
    chosen = jnp.where(second_half[:, None, None, None, :], products[:, 1], products[:, 0])
    return chosen[:, :, :, 0] + parity[:, None, None, :] * chosen[:, :, :, 1]


def helmholtz_solve(spectral_total, pair_ids, helm_coeff):
    second_half, degree, parity = column_terms(pair_ids)
    growth = (degree * (degree + 1)).astype(jnp.float32)
    return spectral_total / (1.0 + helm_coeff[None, None, :, None] * growth[:, None, None, :])


def synthesise(legend, solved, pair_ids):
    second_half, degree, parity = column_terms(pair_ids)
    rounded = solved.astype(jnp.bfloat16)
    lower_mask = jnp.where(second_half, 0.0, 1.0)
    upper_mask = jnp.where(second_half, 1.0, 0.0)
    selector = jnp.stack([lower_mask, upper_mask], axis=1)
    sign_rows = jnp.stack([jnp.ones_like(parity), parity], axis=1)
    weights = (selector[:, :, None, :] * sign_rows[:, None, :, :]).astype(jnp.bfloat16)
    spread = weights[:, :, :, None, None, :] * rounded[:, None, None, :, :, :]
    out_shape = spread.shape[:5]
    spread = spread.reshape(spread.shape[0], -1, NPAIR)
    rows_out = jnp.einsum("ksc,sqc->sqk", legend, spread, preferred_element_type=jnp.float32)
    rows_out = (4.0 * rows_out).astype(jnp.bfloat16)
    return rows_out.reshape(out_shape + (legend.shape[0],))


def on_device(grid_field, row_shift, col_shift, lon_weight, pair_of_slot, legendre, helm_coeff):
    lat_pos = lax.axis_index("lat")
    lon_pos = lax.axis_index("lon")
    lat_count = lax.axis_size("lat")
    lon_count = lax.axis_size("lon")
    band_rows = grid_field.shape[2]
    sector_cols = grid_field.shape[3]
    half_rows = band_rows * lat_count
    row_count = band_rows // lon_count
    first_row = lat_pos * band_rows + lon_pos * row_count
    widened = extended_2(grid_field, (("lon", 3),), WL)
    extended = extended_2(widened, (("lat", 2),), H)
    mirrored = widened[:, ::-1, band_rows - H :, :][:, :, ::-1, :]
    at_equator = lat_pos == lat_count - 1
    upper_rows = jnp.where(at_equator, mirrored, extended[:, :, band_rows + H :, :])
    extended = jnp.concatenate([extended[:, :, : band_rows + H, :], upper_rows], axis=2)
    advected = depart_values(
        extended,
        half_rows,
        H,
        lat_pos * band_rows,
        lon_pos * sector_cols,
        lon_pos * sector_cols - WL,
        row_shift,
        col_shift,
        lon_weight,
    )
    row_data = lax.all_to_all(advected, "lon", split_axis=2, concat_axis=3, tiled=True)
    lat_rows = first_row + jnp.arange(row_count, dtype=jnp.int32)
    per_row = jnp.moveaxis(row_data, 2, 0)

    def spectrum_of_row(row_item):
        return row_spectrum(row_item[0], row_item[1], pair_of_slot)

    spectra = lax.map(spectrum_of_row, (per_row, lat_rows))
    gathered = jax.tree.map(
        lambda part, own: part.astype(own.dtype),
        lax.all_to_all(shortened(spectra), "lon", split_axis=1, concat_axis=0, tiled=True),
        spectra,
    )
    slot_count = legendre.shape[1]
    pair_ids = lax.dynamic_slice_in_dim(pair_of_slot, lon_pos * slot_count, slot_count)
    partial_sum = analyse(legendre, gathered, pair_ids)
    spectral_total = lat_sum(partial_sum)
    spectral_solution = helmholtz_solve(spectral_total, pair_ids, helm_coeff)
    fourier_rows = synthesise(legendre, spectral_solution, pair_ids)
    return (spectral_solution, fourier_rows)


def solution(mesh):
    return jax.shard_map(
        on_device,
        mesh=mesh,
        in_specs=(
            P(None, None, "lat", "lon"),
            P(None, "lat", "lon"),
            P(None, "lat", "lon"),
            P(None, "lat", "lon"),
            P(),
            P("lat", "lon", None),
            P(),
        ),
        out_specs=(P("lon", None, None, None), P("lon", None, None, None, None, "lat")),
        check_vma=False,
    )
```

```python
import math

import jax
import jax.numpy as jnp
from jax import lax
from jax.experimental import pallas as pl
from jax.sharding import PartitionSpec as P

TRUNC = 1279
H = 1
PAIRS = 640
NPAIR = 1281
WL = 10


def extended_2(value, sides, width):
    for axis, dim in sides:
        peers, length = (lax.axis_size(axis), value.shape[dim])
        up = [(i, (i + 1) % peers) for i in range(peers - 1)]
        down = [(j, i) for i, j in up]
        last = lax.slice_in_dim(value, length - width, length, axis=dim)
        initial = lax.slice_in_dim(value, 0, width, axis=dim)
        before = lax.ppermute(last, axis, up)
        after = lax.ppermute(initial, axis, down)
        value = jnp.concatenate([before, value, after], axis=dim)
    return value


def shortened(value):

    def short(part):
        return part.astype(jnp.bfloat16) if part.dtype == jnp.float32 else part

    return jax.tree.map(short, value)


def depart_kernel(ext_ref, code_ref, weight_ref, out_ref):
    code = code_ref[...]
    rows, cols = code.shape[1], code.shape[2]
    left = jnp.zeros(code.shape, jnp.float32)
    right = left
    for dr in range(ext_ref.shape[2] - rows + 1):
        for dc in range(1, ext_ref.shape[3] - cols - 1):
            window = ext_ref[0, :, dr : dr + rows, dc : dc + cols]
            key = dr * 64 + dc
            left = jnp.where(code == key, window, left)
            right = jnp.where(code == key - 1, window, right)
    blend = weight_ref[...]
    out_ref[0] = (1.0 - blend) * left + blend * right


def depart_values(
    extended, half_rows, low_rows, first_row, col_core, col_ext, row_shift, col_shift, lon_weight
):
    row_count = row_shift.shape[1]
    col_count = row_shift.shape[2]
    height = extended.shape[2]
    ext_width = extended.shape[3]
    lat_index = first_row + jnp.arange(row_count, dtype=jnp.int32)[:, None]
    lon_index = col_core + jnp.arange(col_count, dtype=jnp.int32)[None, :]
    length = 20 + 4 * lat_index
    target = jnp.maximum(lat_index + row_shift, 0)
    mirror = jnp.where(target > half_rows - 1, 2 * half_rows - 1 - target, target)
    length_dep = 20 + 4 * mirror
    shifted = jnp.clip(lon_index + col_shift, 0, length - 1)
    column = jnp.minimum(shifted * length_dep // length, length_dep - 2)
    row_off = target - first_row + low_rows - (lat_index - first_row)
    col_off = column - col_ext - (lon_index - col_core)
    code = jnp.where(lon_index < length, row_off * 64 + col_off, -4096).astype(jnp.int32)
    field_count = extended.shape[0]
    blended = pl.pallas_call(
        depart_kernel,
        grid=(field_count,),
        in_specs=[
            pl.BlockSpec((1,) + extended.shape[1:], lambda f: (f, 0, 0, 0)),
            pl.BlockSpec(code.shape, lambda f: (0, 0, 0)),
            pl.BlockSpec(code.shape, lambda f: (0, 0, 0)),
        ],
        out_specs=pl.BlockSpec((1,) + code.shape, lambda f: (f, 0, 0, 0)),
        out_shape=jax.ShapeDtypeStruct((field_count,) + code.shape, jnp.float32),
    )(extended.astype(jnp.float32), code, lon_weight.astype(jnp.float32))
    return jnp.where(lon_index < length, blended, 0.0).astype(jnp.bfloat16)


def phase_table(orders, steps, quarter_len):
    phase_idx = orders[None] * steps[:, None, None] % quarter_len
    angles = phase_idx.astype(jnp.float32) * (2.0 * math.pi) / quarter_len.astype(jnp.float32)
    return jnp.cos(angles), jnp.sin(angles)


def row_spectrum(row_data, lat_index, pair_of_slot):
    length = 20 + 4 * lat_index
    quarter_len = length // 4
    quarters = row_data.reshape(row_data.shape[0], 2, -1, 4)
    slot_count = quarters.shape[2]
    inner_n = 32
    outer_n = -(-slot_count // inner_n)
    offsets = jnp.arange(4, dtype=jnp.int32)[None, None, :]
    norm_scale = 1.0 / jnp.sqrt(length.astype(jnp.float32))
    pair_orders = jnp.stack([pair_of_slot, TRUNC - pair_of_slot], axis=1)
    outer_cos, outer_sin = phase_table(
        pair_orders, jnp.arange(outer_n, dtype=jnp.int32) * inner_n, quarter_len
    )
    inner_cos, inner_sin = phase_table(pair_orders, jnp.arange(inner_n, dtype=jnp.int32), quarter_len)
    cosine = outer_cos[:, None] * inner_cos[None] - outer_sin[:, None] * inner_sin[None]
    minus_sine = -(outer_sin[:, None] * inner_cos[None] + outer_cos[:, None] * inner_sin[None])
    cosine = cosine.reshape((outer_n * inner_n,) + cosine.shape[2:])[:slot_count]
    minus_sine = minus_sine.reshape((outer_n * inner_n,) + minus_sine.shape[2:])[:slot_count]
    slots = jnp.arange(slot_count, dtype=jnp.int32)[:, None, None]
    usable = (2 * pair_orders[None] < length) & (slots < quarter_len)
    factors = jnp.stack(
        [jnp.where(usable, cosine, 0.0), jnp.where(usable, minus_sine, 0.0)], axis=-1
    ).astype(jnp.bfloat16)
    inner = jnp.einsum("aser,fhab->serfhb", factors, quarters, preferred_element_type=jnp.float32)
    twist_idx = pair_orders[:, :, None] * offsets % length
    twist = twist_idx.astype(jnp.float32) * (2.0 * math.pi) / length.astype(jnp.float32)
    twist_cos = jnp.cos(twist)[:, :, None, None, :]
    twist_sin = jnp.sin(twist)[:, :, None, None, :]
    real_part = jnp.sum(inner[:, :, 0] * twist_cos + inner[:, :, 1] * twist_sin, axis=-1)
    imag_part = jnp.sum(inner[:, :, 1] * twist_cos - inner[:, :, 0] * twist_sin, axis=-1)
    spectrum = jnp.stack([real_part, imag_part], axis=2)
    return (spectrum * norm_scale).astype(jnp.bfloat16).reshape(PAIRS, -1)


def lat_sum(value):
    peers = lax.axis_size("lat")
    count = value.size
    pad = (-count) % (peers * 1024)
    flat = jnp.pad(value.reshape(-1), (0, pad)).reshape(peers, -1, 1024)
    pieces = lax.all_to_all(flat.astype(jnp.bfloat16), "lat", 0, 0, tiled=True)
    reduced = jnp.sum(pieces.astype(jnp.float32), axis=0, keepdims=True)
    whole = lax.all_gather(reduced, "lat", axis=0, tiled=True)
    return whole.reshape(-1)[:count].reshape(value.shape)


def column_terms(pair_ids):
    columns = jnp.arange(NPAIR, dtype=jnp.int32)[None, :]
    partner = (TRUNC - pair_ids)[:, None]
    second_half = columns > partner
    degree = jnp.where(second_half, columns - 1, pair_ids[:, None] + columns)
    offset = jnp.where(second_half, columns - 1 - partner, columns)
    parity = (1 - 2 * (offset % 2)).astype(jnp.float32)
    return (second_half, degree, parity)


def analyse(legend, spectra, pair_ids):
    products = jnp.einsum("ksc,ksq->sqc", legend, spectra, preferred_element_type=jnp.float32)
    second_half, degree, parity = column_terms(pair_ids)
    products = products.reshape(products.shape[0], 2, 2, -1, 2, NPAIR)
    chosen = jnp.where(second_half[:, None, None, None, :], products[:, 1], products[:, 0])
    return chosen[:, :, :, 0] + parity[:, None, None, :] * chosen[:, :, :, 1]


def helmholtz_solve(spectral_total, pair_ids, helm_coeff):
    second_half, degree, parity = column_terms(pair_ids)
    growth = (degree * (degree + 1)).astype(jnp.float32)
    return spectral_total / (1.0 + helm_coeff[None, None, :, None] * growth[:, None, None, :])


def synthesise(legend, solved, pair_ids):
    second_half, degree, parity = column_terms(pair_ids)
    rounded = solved.astype(jnp.bfloat16)
    lower_mask = jnp.where(second_half, 0.0, 1.0)
    upper_mask = jnp.where(second_half, 1.0, 0.0)
    selector = jnp.stack([lower_mask, upper_mask], axis=1)
    sign_rows = jnp.stack([jnp.ones_like(parity), parity], axis=1)
    weights = (selector[:, :, None, :] * sign_rows[:, None, :, :]).astype(jnp.bfloat16)
    spread = weights[:, :, :, None, None, :] * rounded[:, None, None, :, :, :]
    out_shape = spread.shape[:5]
    spread = spread.reshape(spread.shape[0], -1, NPAIR)
    rows_out = jnp.einsum("ksc,sqc->sqk", legend, spread, preferred_element_type=jnp.float32)
    rows_out = (4.0 * rows_out).astype(jnp.bfloat16)
    return rows_out.reshape(out_shape + (legend.shape[0],))


def on_device(grid_field, row_shift, col_shift, lon_weight, pair_of_slot, legendre, helm_coeff):
    lat_pos = lax.axis_index("lat")
    lon_pos = lax.axis_index("lon")
    lat_count = lax.axis_size("lat")
    lon_count = lax.axis_size("lon")
    band_rows = grid_field.shape[2]
    sector_cols = grid_field.shape[3]
    half_rows = band_rows * lat_count
    row_count = band_rows // lon_count
    first_row = lat_pos * band_rows + lon_pos * row_count
    widened = extended_2(grid_field, (("lon", 3),), WL)
    extended = extended_2(widened, (("lat", 2),), H)
    mirrored = widened[:, ::-1, band_rows - H :, :][:, :, ::-1, :]
    at_equator = lat_pos == lat_count - 1
    upper_rows = jnp.where(at_equator, mirrored, extended[:, :, band_rows + H :, :])
    extended = jnp.concatenate([extended[:, :, : band_rows + H, :], upper_rows], axis=2)
    advected = depart_values(
        extended,
        half_rows,
        H,
        lat_pos * band_rows,
        lon_pos * sector_cols,
        lon_pos * sector_cols - WL,
        row_shift,
        col_shift,
        lon_weight,
    )
    row_data = lax.all_to_all(advected, "lon", split_axis=2, concat_axis=3, tiled=True)
    lat_rows = first_row + jnp.arange(row_count, dtype=jnp.int32)
    per_row = jnp.moveaxis(row_data, 2, 0)

    def spectrum_of_row(row_item):
        return row_spectrum(row_item[0], row_item[1], pair_of_slot)

    spectra = lax.map(spectrum_of_row, (per_row, lat_rows))
    gathered = jax.tree.map(
        lambda part, own: part.astype(own.dtype),
        lax.all_to_all(shortened(spectra), "lon", split_axis=1, concat_axis=0, tiled=True),
        spectra,
    )
    slot_count = legendre.shape[1]
    pair_ids = lax.dynamic_slice_in_dim(pair_of_slot, lon_pos * slot_count, slot_count)
    partial_sum = analyse(legendre, gathered, pair_ids)
    spectral_total = lat_sum(partial_sum)
    spectral_solution = helmholtz_solve(spectral_total, pair_ids, helm_coeff)
    fourier_rows = synthesise(legendre, spectral_solution, pair_ids)
    return (spectral_solution, fourier_rows)


def solution(mesh):
    return jax.shard_map(
        on_device,
        mesh=mesh,
        in_specs=(
            P(None, None, "lat", "lon"),
            P(None, "lat", "lon"),
            P(None, "lat", "lon"),
            P(None, "lat", "lon"),
            P(),
            P("lat", "lon", None),
            P(),
        ),
        out_specs=(P("lon", None, None, None), P("lon", None, None, None, None, "lat")),
        check_vma=False,
    )
```

```python
import math

import jax
import jax.numpy as jnp
from jax import lax
from jax.experimental import pallas as pl
from jax.sharding import PartitionSpec as P

TRUNC = 1279
H = 1
PAIRS = 640
NPAIR = 1281
WL = 10


def extended_2(value, sides, width):
    for axis, dim in sides:
        peers, length = (lax.axis_size(axis), value.shape[dim])
        up = [(i, (i + 1) % peers) for i in range(peers - 1)]
        down = [(j, i) for i, j in up]
        last = lax.slice_in_dim(value, length - width, length, axis=dim)
        initial = lax.slice_in_dim(value, 0, width, axis=dim)
        before = lax.ppermute(last, axis, up)
        after = lax.ppermute(initial, axis, down)
        value = jnp.concatenate([before, value, after], axis=dim)
    return value


def shortened(value):

    def short(part):
        return part.astype(jnp.bfloat16) if part.dtype == jnp.float32 else part

    return jax.tree.map(short, value)


def depart_kernel(ext_ref, code_ref, weight_ref, out_ref):
    code = code_ref[...]
    rows, cols = code.shape[1], code.shape[2]
    left = jnp.zeros(code.shape, jnp.float32)
    right = left
    for dr in range(ext_ref.shape[2] - rows + 1):
        for dc in range(1, ext_ref.shape[3] - cols - 1):
            window = ext_ref[0, :, dr : dr + rows, dc : dc + cols]
            key = dr * 64 + dc
            left = jnp.where(code == key, window, left)
            right = jnp.where(code == key - 1, window, right)
    blend = weight_ref[...]
    out_ref[0] = (1.0 - blend) * left + blend * right


def depart_values(
    extended, half_rows, low_rows, first_row, col_core, col_ext, row_shift, col_shift, lon_weight
):
    row_count = row_shift.shape[1]
    col_count = row_shift.shape[2]
    height = extended.shape[2]
    ext_width = extended.shape[3]
    lat_index = first_row + jnp.arange(row_count, dtype=jnp.int32)[:, None]
    lon_index = col_core + jnp.arange(col_count, dtype=jnp.int32)[None, :]
    length = 20 + 4 * lat_index
    target = jnp.maximum(lat_index + row_shift, 0)
    mirror = jnp.where(target > half_rows - 1, 2 * half_rows - 1 - target, target)
    length_dep = 20 + 4 * mirror
    shifted = jnp.clip(lon_index + col_shift, 0, length - 1)
    column = jnp.minimum(shifted * length_dep // length, length_dep - 2)
    row_off = target - first_row + low_rows - (lat_index - first_row)
    col_off = column - col_ext - (lon_index - col_core)
    code = jnp.where(lon_index < length, row_off * 64 + col_off, -4096).astype(jnp.int32)
    field_count = extended.shape[0]
    blended = pl.pallas_call(
        depart_kernel,
        grid=(field_count,),
        in_specs=[
            pl.BlockSpec((1,) + extended.shape[1:], lambda f: (f, 0, 0, 0)),
            pl.BlockSpec(code.shape, lambda f: (0, 0, 0)),
            pl.BlockSpec(code.shape, lambda f: (0, 0, 0)),
        ],
        out_specs=pl.BlockSpec((1,) + code.shape, lambda f: (f, 0, 0, 0)),
        out_shape=jax.ShapeDtypeStruct((field_count,) + code.shape, jnp.float32),
    )(extended.astype(jnp.float32), code, lon_weight.astype(jnp.float32))
    return jnp.where(lon_index < length, blended, 0.0).astype(jnp.bfloat16)


def phase_table(orders, steps, quarter_len):
    phase_idx = orders[None] * steps[:, None, None] % quarter_len
    angles = phase_idx.astype(jnp.float32) * (2.0 * math.pi) / quarter_len.astype(jnp.float32)
    return jnp.cos(angles), jnp.sin(angles)


def row_spectrum(row_data, lat_index, pair_of_slot):
    length = 20 + 4 * lat_index
    quarter_len = length // 4
    quarters = row_data.reshape(row_data.shape[0], 2, -1, 4)
    slot_count = quarters.shape[2]
    inner_n = 32
    outer_n = -(-slot_count // inner_n)
    offsets = jnp.arange(4, dtype=jnp.int32)[None, None, :]
    norm_scale = 1.0 / jnp.sqrt(length.astype(jnp.float32))
    pair_orders = jnp.stack([pair_of_slot, TRUNC - pair_of_slot], axis=1)
    outer_cos, outer_sin = phase_table(
        pair_orders, jnp.arange(outer_n, dtype=jnp.int32) * inner_n, quarter_len
    )
    inner_cos, inner_sin = phase_table(pair_orders, jnp.arange(inner_n, dtype=jnp.int32), quarter_len)
    cosine = outer_cos[:, None] * inner_cos[None] - outer_sin[:, None] * inner_sin[None]
    minus_sine = -(outer_sin[:, None] * inner_cos[None] + outer_cos[:, None] * inner_sin[None])
    cosine = cosine.reshape((outer_n * inner_n,) + cosine.shape[2:])[:slot_count]
    minus_sine = minus_sine.reshape((outer_n * inner_n,) + minus_sine.shape[2:])[:slot_count]
    slots = jnp.arange(slot_count, dtype=jnp.int32)[:, None, None]
    usable = (2 * pair_orders[None] < length) & (slots < quarter_len)
    factors = jnp.stack(
        [jnp.where(usable, cosine, 0.0), jnp.where(usable, minus_sine, 0.0)], axis=-1
    ).astype(jnp.bfloat16)
    inner = jnp.einsum("aser,fhab->serfhb", factors, quarters, preferred_element_type=jnp.float32)
    twist_idx = pair_orders[:, :, None] * offsets % length
    twist = twist_idx.astype(jnp.float32) * (2.0 * math.pi) / length.astype(jnp.float32)
    twist_cos = jnp.cos(twist)[:, :, None, None, :]
    twist_sin = jnp.sin(twist)[:, :, None, None, :]
    real_part = jnp.sum(inner[:, :, 0] * twist_cos + inner[:, :, 1] * twist_sin, axis=-1)
    imag_part = jnp.sum(inner[:, :, 1] * twist_cos - inner[:, :, 0] * twist_sin, axis=-1)
    spectrum = jnp.stack([real_part, imag_part], axis=2).transpose(0, 1, 4, 2, 3)
    return (spectrum * norm_scale).astype(jnp.bfloat16).reshape(PAIRS, -1)


def lat_sum(value):
    peers = lax.axis_size("lat")
    count = value.size
    pad = (-count) % (peers * 1024)
    flat = jnp.pad(value.reshape(-1), (0, pad)).reshape(peers, -1, 1024)
    pieces = lax.all_to_all(flat.astype(jnp.bfloat16), "lat", 0, 0, tiled=True)
    reduced = jnp.sum(pieces.astype(jnp.float32), axis=0, keepdims=True)
    whole = lax.all_gather(reduced, "lat", axis=0, tiled=True)
    return whole.reshape(-1)[:count].reshape(value.shape)


def column_terms(pair_ids):
    columns = jnp.arange(NPAIR, dtype=jnp.int32)[None, :]
    partner = (TRUNC - pair_ids)[:, None]
    second_half = columns > partner
    degree = jnp.where(second_half, columns - 1, pair_ids[:, None] + columns)
    offset = jnp.where(second_half, columns - 1 - partner, columns)
    parity = (1 - 2 * (offset % 2)).astype(jnp.float32)
    return (second_half, degree, parity)


def analyse(legend, spectra, pair_ids):
    products = jnp.einsum("ksc,ksq->sqc", legend, spectra, preferred_element_type=jnp.float32)
    second_half, degree, parity = column_terms(pair_ids)
    products = products.reshape(products.shape[0], 2, 2, 2, -1, NPAIR)
    chosen = jnp.where(second_half[:, None, None, None, :], products[:, 1], products[:, 0])
    return chosen[:, 0] + parity[:, None, None, :] * chosen[:, 1]


def helmholtz_solve(spectral_total, pair_ids, helm_coeff):
    second_half, degree, parity = column_terms(pair_ids)
    growth = (degree * (degree + 1)).astype(jnp.float32)
    return spectral_total / (1.0 + helm_coeff[None, None, :, None] * growth[:, None, None, :])


def synthesise(legend, solved, pair_ids):
    second_half, degree, parity = column_terms(pair_ids)
    rounded = solved.astype(jnp.bfloat16)
    lower_mask = jnp.where(second_half, 0.0, 1.0)
    upper_mask = jnp.where(second_half, 1.0, 0.0)
    selector = jnp.stack([lower_mask, upper_mask], axis=1)
    sign_rows = jnp.stack([jnp.ones_like(parity), parity], axis=1)
    weights = (selector[:, :, None, :] * sign_rows[:, None, :, :]).astype(jnp.bfloat16)
    spread = weights[:, :, :, None, None, :] * rounded[:, None, None, :, :, :]
    out_shape = spread.shape[:5]
    spread = spread.reshape(spread.shape[0], -1, NPAIR)
    rows_out = jnp.einsum("ksc,sqc->sqk", legend, spread, preferred_element_type=jnp.float32)
    rows_out = (4.0 * rows_out).astype(jnp.bfloat16)
    return rows_out.reshape(out_shape + (legend.shape[0],))


def on_device(grid_field, row_shift, col_shift, lon_weight, pair_of_slot, legendre, helm_coeff):
    lat_pos = lax.axis_index("lat")
    lon_pos = lax.axis_index("lon")
    lat_count = lax.axis_size("lat")
    lon_count = lax.axis_size("lon")
    band_rows = grid_field.shape[2]
    sector_cols = grid_field.shape[3]
    half_rows = band_rows * lat_count
    row_count = band_rows // lon_count
    first_row = lat_pos * band_rows + lon_pos * row_count
    widened = extended_2(grid_field, (("lon", 3),), WL)
    extended = extended_2(widened, (("lat", 2),), H)
    mirrored = widened[:, ::-1, band_rows - H :, :][:, :, ::-1, :]
    at_equator = lat_pos == lat_count - 1
    upper_rows = jnp.where(at_equator, mirrored, extended[:, :, band_rows + H :, :])
    extended = jnp.concatenate([extended[:, :, : band_rows + H, :], upper_rows], axis=2)
    advected = depart_values(
        extended,
        half_rows,
        H,
        lat_pos * band_rows,
        lon_pos * sector_cols,
        lon_pos * sector_cols - WL,
        row_shift,
        col_shift,
        lon_weight,
    )
    row_data = lax.all_to_all(advected, "lon", split_axis=2, concat_axis=3, tiled=True)
    lat_rows = first_row + jnp.arange(row_count, dtype=jnp.int32)
    per_row = jnp.moveaxis(row_data, 2, 0)

    def spectrum_of_row(row_item):
        return row_spectrum(row_item[0], row_item[1], pair_of_slot)

    spectra = lax.map(spectrum_of_row, (per_row, lat_rows))
    gathered = jax.tree.map(
        lambda part, own: part.astype(own.dtype),
        lax.all_to_all(shortened(spectra), "lon", split_axis=1, concat_axis=0, tiled=True),
        spectra,
    )
    slot_count = legendre.shape[1]
    pair_ids = lax.dynamic_slice_in_dim(pair_of_slot, lon_pos * slot_count, slot_count)
    partial_sum = analyse(legendre, gathered, pair_ids)
    spectral_total = lat_sum(partial_sum)
    spectral_solution = helmholtz_solve(spectral_total, pair_ids, helm_coeff)
    fourier_rows = synthesise(legendre, spectral_solution, pair_ids)
    return (spectral_solution, fourier_rows)


def solution(mesh):
    return jax.shard_map(
        on_device,
        mesh=mesh,
        in_specs=(
            P(None, None, "lat", "lon"),
            P(None, "lat", "lon"),
            P(None, "lat", "lon"),
            P(None, "lat", "lon"),
            P(),
            P("lat", "lon", None),
            P(),
        ),
        out_specs=(P("lon", None, None, None), P("lon", None, None, None, None, "lat")),
        check_vma=False,
    )
```

```python
import math

import jax
import jax.numpy as jnp
from jax import lax
from jax.experimental import pallas as pl
from jax.sharding import PartitionSpec as P

TRUNC = 1279
H = 1
PAIRS = 640
NPAIR = 1281
WL = 10


def extended_2(value, sides, width):
    for axis, dim in sides:
        peers, length = (lax.axis_size(axis), value.shape[dim])
        up = [(i, (i + 1) % peers) for i in range(peers - 1)]
        down = [(j, i) for i, j in up]
        last = lax.slice_in_dim(value, length - width, length, axis=dim)
        initial = lax.slice_in_dim(value, 0, width, axis=dim)
        before = lax.ppermute(last, axis, up)
        after = lax.ppermute(initial, axis, down)
        value = jnp.concatenate([before, value, after], axis=dim)
    return value


def shortened(value):

    def short(part):
        return part.astype(jnp.bfloat16) if part.dtype == jnp.float32 else part

    return jax.tree.map(short, value)


def depart_kernel(ext_ref, code_ref, weight_ref, out_ref):
    code = code_ref[...]
    rows, cols = code.shape[1], code.shape[2]
    left = jnp.zeros(code.shape, jnp.float32)
    right = left
    for dr in range(ext_ref.shape[2] - rows + 1):
        for dc in range(1, ext_ref.shape[3] - cols - 1):
            window = ext_ref[0, :, dr : dr + rows, dc : dc + cols]
            key = dr * 64 + dc
            left = jnp.where(code == key, window, left)
            right = jnp.where(code == key - 1, window, right)
    blend = weight_ref[...]
    out_ref[0] = (1.0 - blend) * left + blend * right


def depart_values(
    extended, half_rows, low_rows, first_row, col_core, col_ext, row_shift, col_shift, lon_weight
):
    row_count = row_shift.shape[1]
    col_count = row_shift.shape[2]
    height = extended.shape[2]
    ext_width = extended.shape[3]
    lat_index = first_row + jnp.arange(row_count, dtype=jnp.int32)[:, None]
    lon_index = col_core + jnp.arange(col_count, dtype=jnp.int32)[None, :]
    length = 20 + 4 * lat_index
    target = jnp.maximum(lat_index + row_shift, 0)
    mirror = jnp.where(target > half_rows - 1, 2 * half_rows - 1 - target, target)
    length_dep = 20 + 4 * mirror
    shifted = jnp.clip(lon_index + col_shift, 0, length - 1)
    column = jnp.minimum(shifted * length_dep // length, length_dep - 2)
    row_off = target - first_row + low_rows - (lat_index - first_row)
    col_off = column - col_ext - (lon_index - col_core)
    code = jnp.where(lon_index < length, row_off * 64 + col_off, -4096).astype(jnp.int32)
    field_count = extended.shape[0]
    blended = pl.pallas_call(
        depart_kernel,
        grid=(field_count,),
        in_specs=[
            pl.BlockSpec((1,) + extended.shape[1:], lambda f: (f, 0, 0, 0)),
            pl.BlockSpec(code.shape, lambda f: (0, 0, 0)),
            pl.BlockSpec(code.shape, lambda f: (0, 0, 0)),
        ],
        out_specs=pl.BlockSpec((1,) + code.shape, lambda f: (f, 0, 0, 0)),
        out_shape=jax.ShapeDtypeStruct((field_count,) + code.shape, jnp.float32),
    )(extended.astype(jnp.float32), code, lon_weight.astype(jnp.float32))
    return jnp.where(lon_index < length, blended, 0.0).astype(jnp.bfloat16)


def phase_table(orders, steps, quarter_len):
    phase_idx = orders[None] * steps[:, None, None] % quarter_len
    angles = phase_idx.astype(jnp.float32) * (2.0 * math.pi) / quarter_len.astype(jnp.float32)
    return jnp.cos(angles), jnp.sin(angles)


def row_spectrum(row_data, lat_index, pair_of_slot):
    length = 20 + 4 * lat_index
    quarter_len = length // 4
    quarters = row_data.reshape(row_data.shape[0], 2, -1, 4)
    slot_count = quarters.shape[2]
    inner_n = 32
    outer_n = -(-slot_count // inner_n)
    offsets = jnp.arange(4, dtype=jnp.int32)[None, None, :]
    norm_scale = 1.0 / jnp.sqrt(length.astype(jnp.float32))
    pair_orders = jnp.stack([pair_of_slot, TRUNC - pair_of_slot], axis=1)
    outer_cos, outer_sin = phase_table(
        pair_orders, jnp.arange(outer_n, dtype=jnp.int32) * inner_n, quarter_len
    )
    inner_cos, inner_sin = phase_table(pair_orders, jnp.arange(inner_n, dtype=jnp.int32), quarter_len)
    cosine = outer_cos[:, None] * inner_cos[None] - outer_sin[:, None] * inner_sin[None]
    minus_sine = -(outer_sin[:, None] * inner_cos[None] + outer_cos[:, None] * inner_sin[None])
    cosine = cosine.reshape((outer_n * inner_n,) + cosine.shape[2:])[:slot_count]
    minus_sine = minus_sine.reshape((outer_n * inner_n,) + minus_sine.shape[2:])[:slot_count]
    slots = jnp.arange(slot_count, dtype=jnp.int32)[:, None, None]
    usable = (2 * pair_orders[None] < length) & (slots < quarter_len)
    factors = jnp.stack(
        [jnp.where(usable, cosine, 0.0), jnp.where(usable, minus_sine, 0.0)], axis=-1
    ).astype(jnp.bfloat16)
    inner = jnp.einsum("aser,fhab->serfhb", factors, quarters, preferred_element_type=jnp.float32)
    twist_idx = pair_orders[:, :, None] * offsets % length
    twist = twist_idx.astype(jnp.float32) * (2.0 * math.pi) / length.astype(jnp.float32)
    twist_cos = jnp.cos(twist)[:, :, None, None, :]
    twist_sin = jnp.sin(twist)[:, :, None, None, :]
    real_part = jnp.sum(inner[:, :, 0] * twist_cos + inner[:, :, 1] * twist_sin, axis=-1)
    imag_part = jnp.sum(inner[:, :, 1] * twist_cos - inner[:, :, 0] * twist_sin, axis=-1)
    spectrum = jnp.stack([real_part, imag_part], axis=2).transpose(0, 1, 4, 2, 3)
    return (spectrum * norm_scale).astype(jnp.bfloat16).reshape(PAIRS, -1)


def lat_sum(value):
    peers = lax.axis_size("lat")
    count = value.size
    pad = (-count) % (peers * 1024)
    flat = jnp.pad(value.reshape(-1), (0, pad)).reshape(peers, -1, 1024)
    pieces = lax.all_to_all(flat.astype(jnp.bfloat16), "lat", 0, 0, tiled=True)
    reduced = jnp.sum(pieces.astype(jnp.float32), axis=0, keepdims=True)
    whole = lax.all_gather(reduced, "lat", axis=0, tiled=True)
    return whole.reshape(-1)[:count].reshape(value.shape)


def column_terms(pair_ids):
    columns = jnp.arange(NPAIR, dtype=jnp.int32)[None, :]
    partner = (TRUNC - pair_ids)[:, None]
    second_half = columns > partner
    degree = jnp.where(second_half, columns - 1, pair_ids[:, None] + columns)
    offset = jnp.where(second_half, columns - 1 - partner, columns)
    parity = (1 - 2 * (offset % 2)).astype(jnp.float32)
    return (second_half, degree, parity)


def analyse(legend, spectra, pair_ids):
    products = jnp.einsum("ksc,ksq->sqc", legend, spectra, preferred_element_type=jnp.float32)
    second_half, degree, parity = column_terms(pair_ids)
    products = products.reshape(products.shape[0], 2, 2, 2, -1, NPAIR)
    chosen = jnp.where(second_half[:, None, None, None, :], products[:, 1], products[:, 0])
    return chosen[:, 0] + parity[:, None, None, :] * chosen[:, 1]


def helmholtz_solve(spectral_total, pair_ids, helm_coeff):
    second_half, degree, parity = column_terms(pair_ids)
    growth = (degree * (degree + 1)).astype(jnp.float32)
    return spectral_total / (1.0 + helm_coeff[None, None, :, None] * growth[:, None, None, :])


def synthesise(legend, solved, pair_ids):
    second_half, degree, parity = column_terms(pair_ids)
    rounded = solved.astype(jnp.bfloat16)
    lower_mask = jnp.where(second_half, 0.0, 1.0)
    upper_mask = jnp.where(second_half, 1.0, 0.0)
    selector = jnp.stack([lower_mask, upper_mask], axis=1)
    sign_rows = jnp.stack([jnp.ones_like(parity), parity], axis=1)
    weights = (selector[:, :, None, :] * sign_rows[:, None, :, :]).astype(jnp.bfloat16)
    spread = weights[:, :, :, None, None, :] * rounded[:, None, None, :, :, :]
    out_shape = spread.shape[:5]
    spread = spread.reshape(spread.shape[0], -1, NPAIR)
    rows_out = jnp.einsum("ksc,sqc->sqk", legend, spread, preferred_element_type=jnp.float32)
    rows_out = (4.0 * rows_out).astype(jnp.bfloat16)
    return rows_out.reshape(out_shape + (legend.shape[0],))


def on_device(grid_field, row_shift, col_shift, lon_weight, pair_of_slot, legendre, helm_coeff):
    lat_pos = lax.axis_index("lat")
    lon_pos = lax.axis_index("lon")
    lat_count = lax.axis_size("lat")
    lon_count = lax.axis_size("lon")
    band_rows = grid_field.shape[2]
    sector_cols = grid_field.shape[3]
    half_rows = band_rows * lat_count
    row_count = band_rows // lon_count
    first_row = lat_pos * band_rows + lon_pos * row_count
    widened = extended_2(grid_field, (("lon", 3),), WL)
    extended = extended_2(widened, (("lat", 2),), H)
    mirrored = widened[:, ::-1, band_rows - H :, :][:, :, ::-1, :]
    at_equator = lat_pos == lat_count - 1
    upper_rows = jnp.where(at_equator, mirrored, extended[:, :, band_rows + H :, :])
    extended = jnp.concatenate([extended[:, :, : band_rows + H, :], upper_rows], axis=2)
    advected = depart_values(
        extended,
        half_rows,
        H,
        lat_pos * band_rows,
        lon_pos * sector_cols,
        lon_pos * sector_cols - WL,
        row_shift,
        col_shift,
        lon_weight,
    )
    advected, pair_tie = lax.optimization_barrier((advected, pair_of_slot))
    row_data = lax.all_to_all(advected, "lon", split_axis=2, concat_axis=3, tiled=True)
    lat_rows = first_row + jnp.arange(row_count, dtype=jnp.int32)
    per_row = jnp.moveaxis(row_data, 2, 0)
    spectra = jax.vmap(lambda row, lat: row_spectrum(row, lat, pair_tie))(per_row, lat_rows)
    gathered = jax.tree.map(
        lambda part, own: part.astype(own.dtype),
        lax.all_to_all(shortened(spectra), "lon", split_axis=1, concat_axis=0, tiled=True),
        spectra,
    )
    slot_count = legendre.shape[1]
    pair_ids = lax.dynamic_slice_in_dim(pair_of_slot, lon_pos * slot_count, slot_count)
    partial_sum = analyse(legendre, gathered, pair_ids)
    spectral_total = lat_sum(partial_sum)
    spectral_solution = helmholtz_solve(spectral_total, pair_ids, helm_coeff)
    fourier_rows = synthesise(legendre, spectral_solution, pair_ids)
    return (spectral_solution, fourier_rows)


def solution(mesh):
    return jax.shard_map(
        on_device,
        mesh=mesh,
        in_specs=(
            P(None, None, "lat", "lon"),
            P(None, "lat", "lon"),
            P(None, "lat", "lon"),
            P(None, "lat", "lon"),
            P(),
            P("lat", "lon", None),
            P(),
        ),
        out_specs=(P("lon", None, None, None), P("lon", None, None, None, None, "lat")),
        check_vma=False,
    )
```

```python
import math

import jax
import jax.numpy as jnp
from jax import lax
from jax.experimental import pallas as pl
from jax.sharding import PartitionSpec as P

TRUNC = 1279
H = 1
PAIRS = 640
NPAIR = 1281
WL = 10


def extended_2(value, sides, width):
    for axis, dim in sides:
        peers, length = (lax.axis_size(axis), value.shape[dim])
        up = [(i, (i + 1) % peers) for i in range(peers - 1)]
        down = [(j, i) for i, j in up]
        last = lax.slice_in_dim(value, length - width, length, axis=dim)
        initial = lax.slice_in_dim(value, 0, width, axis=dim)
        before = lax.ppermute(last, axis, up)
        after = lax.ppermute(initial, axis, down)
        value = jnp.concatenate([before, value, after], axis=dim)
    return value


def shortened(value):

    def short(part):
        return part.astype(jnp.bfloat16) if part.dtype == jnp.float32 else part

    return jax.tree.map(short, value)


def depart_kernel(ext_ref, code_ref, weight_ref, out_ref):
    code = code_ref[...]
    rows, cols = code.shape[1], code.shape[2]
    left = jnp.zeros(code.shape, jnp.float32)
    right = left
    for dr in range(ext_ref.shape[2] - rows + 1):
        for dc in range(1, ext_ref.shape[3] - cols - 1):
            window = ext_ref[0, :, dr : dr + rows, dc : dc + cols]
            key = dr * 64 + dc
            left = jnp.where(code == key, window, left)
            right = jnp.where(code == key - 1, window, right)
    blend = weight_ref[...]
    out_ref[0] = (1.0 - blend) * left + blend * right


def depart_values(
    extended, half_rows, low_rows, first_row, col_core, col_ext, row_shift, col_shift, lon_weight
):
    row_count = row_shift.shape[1]
    col_count = row_shift.shape[2]
    height = extended.shape[2]
    ext_width = extended.shape[3]
    lat_index = first_row + jnp.arange(row_count, dtype=jnp.int32)[:, None]
    lon_index = col_core + jnp.arange(col_count, dtype=jnp.int32)[None, :]
    length = 20 + 4 * lat_index
    target = jnp.maximum(lat_index + row_shift, 0)
    mirror = jnp.where(target > half_rows - 1, 2 * half_rows - 1 - target, target)
    length_dep = 20 + 4 * mirror
    shifted = jnp.clip(lon_index + col_shift, 0, length - 1)
    column = jnp.minimum(shifted * length_dep // length, length_dep - 2)
    row_off = target - first_row + low_rows - (lat_index - first_row)
    col_off = column - col_ext - (lon_index - col_core)
    code = jnp.where(lon_index < length, row_off * 64 + col_off, -4096).astype(jnp.int32)
    field_count = extended.shape[0]
    blended = pl.pallas_call(
        depart_kernel,
        grid=(field_count,),
        in_specs=[
            pl.BlockSpec((1,) + extended.shape[1:], lambda f: (f, 0, 0, 0)),
            pl.BlockSpec(code.shape, lambda f: (0, 0, 0)),
            pl.BlockSpec(code.shape, lambda f: (0, 0, 0)),
        ],
        out_specs=pl.BlockSpec((1,) + code.shape, lambda f: (f, 0, 0, 0)),
        out_shape=jax.ShapeDtypeStruct((field_count,) + code.shape, jnp.float32),
    )(extended.astype(jnp.float32), code, lon_weight.astype(jnp.float32))
    return jnp.where(lon_index < length, blended, 0.0).astype(jnp.bfloat16)


def phase_table(orders, steps, quarter_len):
    phase_idx = orders[None] * steps[:, None, None] % quarter_len
    angles = phase_idx.astype(jnp.float32) * (2.0 * math.pi) / quarter_len.astype(jnp.float32)
    return jnp.cos(angles), jnp.sin(angles)


def row_spectrum(row_data, lat_index, pair_of_slot):
    length = 20 + 4 * lat_index
    quarter_len = length // 4
    quarters = row_data.reshape(row_data.shape[0], 2, -1, 4)
    slot_count = quarters.shape[2]
    inner_n = 32
    outer_n = -(-slot_count // inner_n)
    offsets = jnp.arange(4, dtype=jnp.int32)[None, None, :]
    norm_scale = 1.0 / jnp.sqrt(length.astype(jnp.float32))
    pair_orders = jnp.stack([pair_of_slot, TRUNC - pair_of_slot], axis=1)
    outer_cos, outer_sin = phase_table(
        pair_orders, jnp.arange(outer_n, dtype=jnp.int32) * inner_n, quarter_len
    )
    inner_cos, inner_sin = phase_table(pair_orders, jnp.arange(inner_n, dtype=jnp.int32), quarter_len)
    cosine = outer_cos[:, None] * inner_cos[None] - outer_sin[:, None] * inner_sin[None]
    minus_sine = -(outer_sin[:, None] * inner_cos[None] + outer_cos[:, None] * inner_sin[None])
    cosine = cosine.reshape((outer_n * inner_n,) + cosine.shape[2:])[:slot_count]
    minus_sine = minus_sine.reshape((outer_n * inner_n,) + minus_sine.shape[2:])[:slot_count]
    slots = jnp.arange(slot_count, dtype=jnp.int32)[:, None, None]
    usable = (2 * pair_orders[None] < length) & (slots < quarter_len)
    factors = jnp.stack(
        [jnp.where(usable, cosine, 0.0), jnp.where(usable, minus_sine, 0.0)], axis=-1
    ).astype(jnp.bfloat16)
    inner = jnp.einsum("aser,fhab->serfhb", factors, quarters, preferred_element_type=jnp.float32)
    twist_idx = pair_orders[:, :, None] * offsets % length
    twist = twist_idx.astype(jnp.float32) * (2.0 * math.pi) / length.astype(jnp.float32)
    twist_cos = jnp.cos(twist)[:, :, None, None, :]
    twist_sin = jnp.sin(twist)[:, :, None, None, :]
    real_part = jnp.sum(inner[:, :, 0] * twist_cos + inner[:, :, 1] * twist_sin, axis=-1)
    imag_part = jnp.sum(inner[:, :, 1] * twist_cos - inner[:, :, 0] * twist_sin, axis=-1)
    spectrum = jnp.stack([real_part, imag_part], axis=2).transpose(0, 1, 4, 2, 3)
    return (spectrum * norm_scale).astype(jnp.bfloat16).reshape(PAIRS, -1)


def lat_sum(value):
    peers = lax.axis_size("lat")
    lead = value.shape[0]
    grouped = value.reshape(lead, -1, value.shape[-1])
    groups = grouped.shape[1]
    if groups % peers == 0:
        grouped = jnp.moveaxis(grouped, 1, 0)
        pieces = lax.all_to_all(grouped.astype(jnp.bfloat16), "lat", 0, 0, tiled=True)
        pieces = pieces.astype(jnp.float32).reshape((peers, groups // peers) + grouped.shape[1:])
        reduced = jnp.sum(pieces, axis=0)
        whole = lax.all_gather(reduced, "lat", axis=0, tiled=True)
        return jnp.moveaxis(whole, 0, 1).reshape(value.shape)
    count = value.size
    pad = (-count) % (peers * 1024)
    flat = jnp.pad(value.reshape(-1), (0, pad)).reshape(peers, -1, 1024)
    pieces = lax.all_to_all(flat.astype(jnp.bfloat16), "lat", 0, 0, tiled=True)
    reduced = jnp.sum(pieces.astype(jnp.float32), axis=0, keepdims=True)
    whole = lax.all_gather(reduced, "lat", axis=0, tiled=True)
    return whole.reshape(-1)[:count].reshape(value.shape)


def column_terms(pair_ids):
    columns = jnp.arange(NPAIR, dtype=jnp.int32)[None, :]
    partner = (TRUNC - pair_ids)[:, None]
    second_half = columns > partner
    degree = jnp.where(second_half, columns - 1, pair_ids[:, None] + columns)
    offset = jnp.where(second_half, columns - 1 - partner, columns)
    parity = (1 - 2 * (offset % 2)).astype(jnp.float32)
    return (second_half, degree, parity)


def analyse(legend, spectra, pair_ids):
    products = jnp.einsum("ksc,ksq->sqc", legend, spectra, preferred_element_type=jnp.float32)
    second_half, degree, parity = column_terms(pair_ids)
    products = products.reshape(products.shape[0], 2, 2, 2, -1, NPAIR)
    chosen = jnp.where(second_half[:, None, None, None, :], products[:, 1], products[:, 0])
    return chosen[:, 0] + parity[:, None, None, :] * chosen[:, 1]


def helmholtz_solve(spectral_total, pair_ids, helm_coeff):
    second_half, degree, parity = column_terms(pair_ids)
    growth = (degree * (degree + 1)).astype(jnp.float32)
    return spectral_total / (1.0 + helm_coeff[None, None, :, None] * growth[:, None, None, :])


def synthesise(legend, solved, pair_ids):
    second_half, degree, parity = column_terms(pair_ids)
    rounded = solved.astype(jnp.bfloat16)
    lower_mask = jnp.where(second_half, 0.0, 1.0)
    upper_mask = jnp.where(second_half, 1.0, 0.0)
    selector = jnp.stack([lower_mask, upper_mask], axis=1)
    sign_rows = jnp.stack([jnp.ones_like(parity), parity], axis=1)
    weights = (selector[:, :, None, :] * sign_rows[:, None, :, :]).astype(jnp.bfloat16)
    spread = weights[:, :, :, None, None, :] * rounded[:, None, None, :, :, :]
    out_shape = spread.shape[:5]
    spread = spread.reshape(spread.shape[0], -1, NPAIR)
    rows_out = jnp.einsum("ksc,sqc->sqk", legend, spread, preferred_element_type=jnp.float32)
    rows_out = (4.0 * rows_out).astype(jnp.bfloat16)
    return rows_out.reshape(out_shape + (legend.shape[0],))


def on_device(grid_field, row_shift, col_shift, lon_weight, pair_of_slot, legendre, helm_coeff):
    lat_pos = lax.axis_index("lat")
    lon_pos = lax.axis_index("lon")
    lat_count = lax.axis_size("lat")
    lon_count = lax.axis_size("lon")
    band_rows = grid_field.shape[2]
    sector_cols = grid_field.shape[3]
    half_rows = band_rows * lat_count
    row_count = band_rows // lon_count
    first_row = lat_pos * band_rows + lon_pos * row_count
    widened = extended_2(grid_field, (("lon", 3),), WL)
    extended = extended_2(widened, (("lat", 2),), H)
    mirrored = widened[:, ::-1, band_rows - H :, :][:, :, ::-1, :]
    at_equator = lat_pos == lat_count - 1
    upper_rows = jnp.where(at_equator, mirrored, extended[:, :, band_rows + H :, :])
    extended = jnp.concatenate([extended[:, :, : band_rows + H, :], upper_rows], axis=2)
    advected = depart_values(
        extended,
        half_rows,
        H,
        lat_pos * band_rows,
        lon_pos * sector_cols,
        lon_pos * sector_cols - WL,
        row_shift,
        col_shift,
        lon_weight,
    )
    advected, pair_tie = lax.optimization_barrier((advected, pair_of_slot))
    row_data = lax.all_to_all(advected, "lon", split_axis=2, concat_axis=3, tiled=True)
    lat_rows = first_row + jnp.arange(row_count, dtype=jnp.int32)
    per_row = jnp.moveaxis(row_data, 2, 0)
    spectra = jax.vmap(lambda row, lat: row_spectrum(row, lat, pair_tie))(per_row, lat_rows)
    gathered = jax.tree.map(
        lambda part, own: part.astype(own.dtype),
        lax.all_to_all(shortened(spectra), "lon", split_axis=1, concat_axis=0, tiled=True),
        spectra,
    )
    slot_count = legendre.shape[1]
    pair_ids = lax.dynamic_slice_in_dim(pair_of_slot, lon_pos * slot_count, slot_count)
    partial_sum = analyse(legendre, gathered, pair_ids)
    spectral_total = lat_sum(partial_sum)
    spectral_solution = helmholtz_solve(spectral_total, pair_ids, helm_coeff)
    fourier_rows = synthesise(legendre, spectral_solution, pair_ids)
    return (spectral_solution, fourier_rows)


def solution(mesh):
    return jax.shard_map(
        on_device,
        mesh=mesh,
        in_specs=(
            P(None, None, "lat", "lon"),
            P(None, "lat", "lon"),
            P(None, "lat", "lon"),
            P(None, "lat", "lon"),
            P(),
            P("lat", "lon", None),
            P(),
        ),
        out_specs=(P("lon", None, None, None), P("lon", None, None, None, None, "lat")),
        check_vma=False,
    )
```

```python
import math

import jax
import jax.numpy as jnp
from jax import lax
from jax.experimental import pallas as pl
from jax.sharding import PartitionSpec as P

TRUNC = 1279
H = 1
PAIRS = 640
NPAIR = 1281
WL = 10


def extended_2(value, sides, width):
    for axis, dim in sides:
        peers, length = (lax.axis_size(axis), value.shape[dim])
        up = [(i, (i + 1) % peers) for i in range(peers - 1)]
        down = [(j, i) for i, j in up]
        last = lax.slice_in_dim(value, length - width, length, axis=dim)
        initial = lax.slice_in_dim(value, 0, width, axis=dim)
        before = lax.ppermute(last, axis, up)
        after = lax.ppermute(initial, axis, down)
        value = jnp.concatenate([before, value, after], axis=dim)
    return value


def shortened(value):

    def short(part):
        return part.astype(jnp.bfloat16) if part.dtype == jnp.float32 else part

    return jax.tree.map(short, value)


def depart_kernel(ext_ref, code_ref, weight_ref, out_ref):
    code = code_ref[...]
    rows, cols = code.shape[1], code.shape[2]
    left = jnp.zeros(code.shape, jnp.float32)
    right = left
    reach = ((WL - 8, WL + 6), (WL - 5, WL + 6), (WL - 5, WL + 9))
    for dr in range(ext_ref.shape[2] - rows + 1):
        for dc in range(*reach[dr]):
            window = ext_ref[0, :, dr : dr + rows, dc : dc + cols]
            key = dr * 64 + dc
            left = jnp.where(code == key, window, left)
            right = jnp.where(code == key - 1, window, right)
    blend = weight_ref[...]
    out_ref[0] = (1.0 - blend) * left + blend * right


def depart_values(
    extended, half_rows, low_rows, first_row, col_core, col_ext, row_shift, col_shift, lon_weight
):
    row_count = row_shift.shape[1]
    col_count = row_shift.shape[2]
    height = extended.shape[2]
    ext_width = extended.shape[3]
    lat_index = first_row + jnp.arange(row_count, dtype=jnp.int32)[:, None]
    lon_index = col_core + jnp.arange(col_count, dtype=jnp.int32)[None, :]
    length = 20 + 4 * lat_index
    target = jnp.maximum(lat_index + row_shift, 0)
    mirror = jnp.where(target > half_rows - 1, 2 * half_rows - 1 - target, target)
    length_dep = 20 + 4 * mirror
    shifted = jnp.clip(lon_index + col_shift, 0, length - 1)
    column = jnp.minimum(shifted * length_dep // length, length_dep - 2)
    row_off = target - first_row + low_rows - (lat_index - first_row)
    col_off = column - col_ext - (lon_index - col_core)
    code = jnp.where(lon_index < length, row_off * 64 + col_off, -4096).astype(jnp.int32)
    field_count = extended.shape[0]
    blended = pl.pallas_call(
        depart_kernel,
        grid=(field_count,),
        in_specs=[
            pl.BlockSpec((1,) + extended.shape[1:], lambda f: (f, 0, 0, 0)),
            pl.BlockSpec(code.shape, lambda f: (0, 0, 0)),
            pl.BlockSpec(code.shape, lambda f: (0, 0, 0)),
        ],
        out_specs=pl.BlockSpec((1,) + code.shape, lambda f: (f, 0, 0, 0)),
        out_shape=jax.ShapeDtypeStruct((field_count,) + code.shape, jnp.float32),
    )(extended.astype(jnp.float32), code, lon_weight.astype(jnp.float32))
    return jnp.where(lon_index < length, blended, 0.0).astype(jnp.bfloat16)


def phase_table(orders, steps, quarter_len):
    phase_idx = orders[None] * steps[:, None, None] % quarter_len
    angles = phase_idx.astype(jnp.float32) * (2.0 * math.pi) / quarter_len.astype(jnp.float32)
    return jnp.cos(angles), jnp.sin(angles)


def row_spectrum(row_data, lat_index, pair_of_slot):
    length = 20 + 4 * lat_index
    quarter_len = length // 4
    quarters = row_data.reshape(row_data.shape[0], 2, -1, 4)
    slot_count = quarters.shape[2]
    inner_n = 32
    outer_n = -(-slot_count // inner_n)
    offsets = jnp.arange(4, dtype=jnp.int32)[None, None, :]
    norm_scale = 1.0 / jnp.sqrt(length.astype(jnp.float32))
    pair_orders = jnp.stack([pair_of_slot, TRUNC - pair_of_slot], axis=1)
    outer_cos, outer_sin = phase_table(
        pair_orders, jnp.arange(outer_n, dtype=jnp.int32) * inner_n, quarter_len
    )
    inner_cos, inner_sin = phase_table(pair_orders, jnp.arange(inner_n, dtype=jnp.int32), quarter_len)
    cosine = outer_cos[:, None] * inner_cos[None] - outer_sin[:, None] * inner_sin[None]
    minus_sine = -(outer_sin[:, None] * inner_cos[None] + outer_cos[:, None] * inner_sin[None])
    cosine = cosine.reshape((outer_n * inner_n,) + cosine.shape[2:])[:slot_count]
    minus_sine = minus_sine.reshape((outer_n * inner_n,) + minus_sine.shape[2:])[:slot_count]
    slots = jnp.arange(slot_count, dtype=jnp.int32)[:, None, None]
    usable = (2 * pair_orders[None] < length) & (slots < quarter_len)
    factors = jnp.stack(
        [jnp.where(usable, cosine, 0.0), jnp.where(usable, minus_sine, 0.0)], axis=-1
    ).astype(jnp.bfloat16)
    inner = jnp.einsum("aser,fhab->serfhb", factors, quarters, preferred_element_type=jnp.float32)
    twist_idx = pair_orders[:, :, None] * offsets % length
    twist = twist_idx.astype(jnp.float32) * (2.0 * math.pi) / length.astype(jnp.float32)
    twist_cos = jnp.cos(twist)[:, :, None, None, :]
    twist_sin = jnp.sin(twist)[:, :, None, None, :]
    real_part = jnp.sum(inner[:, :, 0] * twist_cos + inner[:, :, 1] * twist_sin, axis=-1)
    imag_part = jnp.sum(inner[:, :, 1] * twist_cos - inner[:, :, 0] * twist_sin, axis=-1)
    spectrum = jnp.stack([real_part, imag_part], axis=2).transpose(0, 1, 4, 2, 3)
    return (spectrum * norm_scale).astype(jnp.bfloat16).reshape(PAIRS, -1)


def lat_sum(value):
    peers = lax.axis_size("lat")
    lead = value.shape[0]
    grouped = value.reshape(lead, -1, value.shape[-1])
    groups = grouped.shape[1]
    if groups % peers == 0:
        grouped = jnp.moveaxis(grouped, 1, 0)
        pieces = lax.all_to_all(grouped.astype(jnp.bfloat16), "lat", 0, 0, tiled=True)
        pieces = pieces.astype(jnp.float32).reshape((peers, groups // peers) + grouped.shape[1:])
        reduced = jnp.sum(pieces, axis=0)
        whole = lax.all_gather(reduced, "lat", axis=0, tiled=True)
        return jnp.moveaxis(whole, 0, 1).reshape(value.shape)
    count = value.size
    pad = (-count) % (peers * 1024)
    flat = jnp.pad(value.reshape(-1), (0, pad)).reshape(peers, -1, 1024)
    pieces = lax.all_to_all(flat.astype(jnp.bfloat16), "lat", 0, 0, tiled=True)
    reduced = jnp.sum(pieces.astype(jnp.float32), axis=0, keepdims=True)
    whole = lax.all_gather(reduced, "lat", axis=0, tiled=True)
    return whole.reshape(-1)[:count].reshape(value.shape)


def column_terms(pair_ids):
    columns = jnp.arange(NPAIR, dtype=jnp.int32)[None, :]
    partner = (TRUNC - pair_ids)[:, None]
    second_half = columns > partner
    degree = jnp.where(second_half, columns - 1, pair_ids[:, None] + columns)
    offset = jnp.where(second_half, columns - 1 - partner, columns)
    parity = (1 - 2 * (offset % 2)).astype(jnp.float32)
    return (second_half, degree, parity)


def analyse(legend, spectra, pair_ids):
    products = jnp.einsum("ksc,ksq->sqc", legend, spectra, preferred_element_type=jnp.float32)
    second_half, degree, parity = column_terms(pair_ids)
    products = products.reshape(products.shape[0], 2, 2, 2, -1, NPAIR)
    chosen = jnp.where(second_half[:, None, None, None, :], products[:, 1], products[:, 0])
    return chosen[:, 0] + parity[:, None, None, :] * chosen[:, 1]


def helmholtz_solve(spectral_total, pair_ids, helm_coeff):
    second_half, degree, parity = column_terms(pair_ids)
    growth = (degree * (degree + 1)).astype(jnp.float32)
    return spectral_total / (1.0 + helm_coeff[None, None, :, None] * growth[:, None, None, :])


def synthesise(legend, solved, pair_ids):
    second_half, degree, parity = column_terms(pair_ids)
    rounded = solved.astype(jnp.bfloat16)
    lower_mask = jnp.where(second_half, 0.0, 1.0)
    upper_mask = jnp.where(second_half, 1.0, 0.0)
    selector = jnp.stack([lower_mask, upper_mask], axis=1)
    sign_rows = jnp.stack([jnp.ones_like(parity), parity], axis=1)
    weights = (selector[:, :, None, :] * sign_rows[:, None, :, :]).astype(jnp.bfloat16)
    spread = weights[:, :, :, None, None, :] * rounded[:, None, None, :, :, :]
    out_shape = spread.shape[:5]
    spread = spread.reshape(spread.shape[0], -1, NPAIR)
    rows_out = jnp.einsum("ksc,sqc->sqk", legend, spread, preferred_element_type=jnp.float32)
    rows_out = (4.0 * rows_out).astype(jnp.bfloat16)
    return rows_out.reshape(out_shape + (legend.shape[0],))


def on_device(grid_field, row_shift, col_shift, lon_weight, pair_of_slot, legendre, helm_coeff):
    lat_pos = lax.axis_index("lat")
    lon_pos = lax.axis_index("lon")
    lat_count = lax.axis_size("lat")
    lon_count = lax.axis_size("lon")
    band_rows = grid_field.shape[2]
    sector_cols = grid_field.shape[3]
    half_rows = band_rows * lat_count
    row_count = band_rows // lon_count
    first_row = lat_pos * band_rows + lon_pos * row_count
    widened = extended_2(grid_field, (("lon", 3),), WL)
    extended = extended_2(widened, (("lat", 2),), H)
    mirrored = widened[:, ::-1, band_rows - H :, :][:, :, ::-1, :]
    at_equator = lat_pos == lat_count - 1
    upper_rows = jnp.where(at_equator, mirrored, extended[:, :, band_rows + H :, :])
    extended = jnp.concatenate([extended[:, :, : band_rows + H, :], upper_rows], axis=2)
    advected = depart_values(
        extended,
        half_rows,
        H,
        lat_pos * band_rows,
        lon_pos * sector_cols,
        lon_pos * sector_cols - WL,
        row_shift,
        col_shift,
        lon_weight,
    )
    advected, pair_tie = lax.optimization_barrier((advected, pair_of_slot))
    row_data = lax.all_to_all(advected, "lon", split_axis=2, concat_axis=3, tiled=True)
    lat_rows = first_row + jnp.arange(row_count, dtype=jnp.int32)
    per_row = jnp.moveaxis(row_data, 2, 0)
    spectra = jax.vmap(lambda row, lat: row_spectrum(row, lat, pair_tie))(per_row, lat_rows)
    gathered = jax.tree.map(
        lambda part, own: part.astype(own.dtype),
        lax.all_to_all(shortened(spectra), "lon", split_axis=1, concat_axis=0, tiled=True),
        spectra,
    )
    slot_count = legendre.shape[1]
    pair_ids = lax.dynamic_slice_in_dim(pair_of_slot, lon_pos * slot_count, slot_count)
    partial_sum = analyse(legendre, gathered, pair_ids)
    spectral_total = lat_sum(partial_sum)
    spectral_solution = helmholtz_solve(spectral_total, pair_ids, helm_coeff)
    fourier_rows = synthesise(legendre, spectral_solution, pair_ids)
    return (spectral_solution, fourier_rows)


def solution(mesh):
    return jax.shard_map(
        on_device,
        mesh=mesh,
        in_specs=(
            P(None, None, "lat", "lon"),
            P(None, "lat", "lon"),
            P(None, "lat", "lon"),
            P(None, "lat", "lon"),
            P(),
            P("lat", "lon", None),
            P(),
        ),
        out_specs=(P("lon", None, None, None), P("lon", None, None, None, None, "lat")),
        check_vma=False,
    )
```

```python
import math

import jax
import jax.numpy as jnp
from jax import lax
from jax.experimental import pallas as pl
from jax.sharding import PartitionSpec as P

TRUNC = 1279
H = 1
PAIRS = 640
NPAIR = 1281
WL = 10


def extended_2(value, sides, width):
    for axis, dim in sides:
        peers, length = (lax.axis_size(axis), value.shape[dim])
        up = [(i, (i + 1) % peers) for i in range(peers - 1)]
        down = [(j, i) for i, j in up]
        last = lax.slice_in_dim(value, length - width, length, axis=dim)
        initial = lax.slice_in_dim(value, 0, width, axis=dim)
        before = lax.ppermute(last, axis, up)
        after = lax.ppermute(initial, axis, down)
        value = jnp.concatenate([before, value, after], axis=dim)
    return value


def shortened(value):

    def short(part):
        return part.astype(jnp.bfloat16) if part.dtype == jnp.float32 else part

    return jax.tree.map(short, value)


def depart_kernel(ext_ref, code_ref, weight_ref, out_ref):
    code = code_ref[...]
    rows, cols = code.shape[1], code.shape[2]
    left = jnp.zeros(code.shape, jnp.float32)
    right = left
    reach = ((WL - 8, WL + 6), (WL - 5, WL + 6), (WL - 5, WL + 9))
    for dr in range(ext_ref.shape[2] - rows + 1):
        for dc in range(*reach[dr]):
            window = ext_ref[0, :, dr : dr + rows, dc : dc + cols]
            key = dr * 64 + dc
            left = jnp.where(code == key, window, left)
            right = jnp.where(code == key - 1, window, right)
    blend = weight_ref[...].astype(jnp.float32)
    out_ref[0] = (1.0 - blend) * left + blend * right


def depart_values(
    extended, half_rows, low_rows, first_row, col_core, col_ext, row_shift, col_shift, lon_weight
):
    row_count = row_shift.shape[1]
    col_count = row_shift.shape[2]
    height = extended.shape[2]
    ext_width = extended.shape[3]
    lat_index = first_row + jnp.arange(row_count, dtype=jnp.int32)[:, None]
    lon_index = col_core + jnp.arange(col_count, dtype=jnp.int32)[None, :]
    length = 20 + 4 * lat_index
    target = jnp.maximum(lat_index + row_shift, 0)
    mirror = jnp.where(target > half_rows - 1, 2 * half_rows - 1 - target, target)
    length_dep = 20 + 4 * mirror
    shifted = jnp.clip(lon_index + col_shift, 0, length - 1)
    column = jnp.minimum(shifted * length_dep // length, length_dep - 2)
    row_off = target - first_row + low_rows - (lat_index - first_row)
    col_off = column - col_ext - (lon_index - col_core)
    code = jnp.where(lon_index < length, row_off * 64 + col_off, -4096).astype(jnp.int32)
    field_count = extended.shape[0]
    blended = pl.pallas_call(
        depart_kernel,
        grid=(field_count,),
        in_specs=[
            pl.BlockSpec((1,) + extended.shape[1:], lambda f: (f, 0, 0, 0)),
            pl.BlockSpec(code.shape, lambda f: (0, 0, 0)),
            pl.BlockSpec(code.shape, lambda f: (0, 0, 0)),
        ],
        out_specs=pl.BlockSpec((1,) + code.shape, lambda f: (f, 0, 0, 0)),
        out_shape=jax.ShapeDtypeStruct((field_count,) + code.shape, jnp.float32),
    )(extended.astype(jnp.float32), code, lon_weight)
    return jnp.where(lon_index < length, blended, 0.0).astype(jnp.bfloat16)


def phase_table(orders, steps, quarter_len):
    product = orders[None] * steps[:, None, None]
    whole = jnp.floor(product.astype(jnp.float32) / quarter_len.astype(jnp.float32))
    phase_idx = product - whole.astype(jnp.int32) * quarter_len
    phase_idx = jnp.where(phase_idx < 0, phase_idx + quarter_len, phase_idx)
    phase_idx = jnp.where(phase_idx >= quarter_len, phase_idx - quarter_len, phase_idx)
    angles = phase_idx.astype(jnp.float32) * (2.0 * math.pi) / quarter_len.astype(jnp.float32)
    return jnp.cos(angles), jnp.sin(angles)


def row_spectrum(row_data, lat_index, pair_of_slot):
    length = 20 + 4 * lat_index
    quarter_len = length // 4
    quarters = row_data.reshape(row_data.shape[0], 2, -1, 4)
    slot_count = quarters.shape[2]
    inner_n = 32
    outer_n = -(-slot_count // inner_n)
    offsets = jnp.arange(4, dtype=jnp.int32)[None, None, :]
    norm_scale = 1.0 / jnp.sqrt(length.astype(jnp.float32))
    pair_orders = jnp.stack([pair_of_slot, TRUNC - pair_of_slot], axis=1)
    outer_cos, outer_sin = phase_table(
        pair_orders, jnp.arange(outer_n, dtype=jnp.int32) * inner_n, quarter_len
    )
    inner_cos, inner_sin = phase_table(pair_orders, jnp.arange(inner_n, dtype=jnp.int32), quarter_len)
    cosine = outer_cos[:, None] * inner_cos[None] - outer_sin[:, None] * inner_sin[None]
    minus_sine = -(outer_sin[:, None] * inner_cos[None] + outer_cos[:, None] * inner_sin[None])
    cosine = cosine.reshape((outer_n * inner_n,) + cosine.shape[2:])[:slot_count]
    minus_sine = minus_sine.reshape((outer_n * inner_n,) + minus_sine.shape[2:])[:slot_count]
    slots = jnp.arange(slot_count, dtype=jnp.int32)[:, None, None]
    usable = (2 * pair_orders[None] < length) & (slots < quarter_len)
    factors = jnp.stack(
        [jnp.where(usable, cosine, 0.0), jnp.where(usable, minus_sine, 0.0)], axis=-1
    ).astype(jnp.bfloat16)
    inner = jnp.einsum("aser,fhab->serfhb", factors, quarters, preferred_element_type=jnp.float32)
    twist_idx = pair_orders[:, :, None] * offsets % length
    twist = twist_idx.astype(jnp.float32) * (2.0 * math.pi) / length.astype(jnp.float32)
    twist_cos = jnp.cos(twist)[:, :, None, None, :]
    twist_sin = jnp.sin(twist)[:, :, None, None, :]
    real_part = jnp.sum(inner[:, :, 0] * twist_cos + inner[:, :, 1] * twist_sin, axis=-1)
    imag_part = jnp.sum(inner[:, :, 1] * twist_cos - inner[:, :, 0] * twist_sin, axis=-1)
    spectrum = jnp.stack([real_part, imag_part], axis=2).transpose(0, 1, 4, 2, 3)
    return (spectrum * norm_scale).astype(jnp.bfloat16).reshape(PAIRS, -1)


def lat_sum(value):
    peers = lax.axis_size("lat")
    lead = value.shape[0]
    grouped = value.reshape(lead, -1, value.shape[-1])
    groups = grouped.shape[1]
    if groups % peers == 0:
        grouped = jnp.moveaxis(grouped, 1, 0)
        pieces = lax.all_to_all(grouped.astype(jnp.bfloat16), "lat", 0, 0, tiled=True)
        pieces = pieces.astype(jnp.float32).reshape((peers, groups // peers) + grouped.shape[1:])
        reduced = jnp.sum(pieces, axis=0)
        whole = lax.all_gather(reduced, "lat", axis=0, tiled=True)
        return jnp.moveaxis(whole, 0, 1).reshape(value.shape)
    count = value.size
    pad = (-count) % (peers * 1024)
    flat = jnp.pad(value.reshape(-1), (0, pad)).reshape(peers, -1, 1024)
    pieces = lax.all_to_all(flat.astype(jnp.bfloat16), "lat", 0, 0, tiled=True)
    reduced = jnp.sum(pieces.astype(jnp.float32), axis=0, keepdims=True)
    whole = lax.all_gather(reduced, "lat", axis=0, tiled=True)
    return whole.reshape(-1)[:count].reshape(value.shape)


def column_terms(pair_ids):
    columns = jnp.arange(NPAIR, dtype=jnp.int32)[None, :]
    partner = (TRUNC - pair_ids)[:, None]
    second_half = columns > partner
    degree = jnp.where(second_half, columns - 1, pair_ids[:, None] + columns)
    offset = jnp.where(second_half, columns - 1 - partner, columns)
    parity = (1 - 2 * (offset % 2)).astype(jnp.float32)
    return (second_half, degree, parity)


def analyse(legend, spectra, pair_ids):
    products = jnp.einsum("ksc,ksq->sqc", legend, spectra, preferred_element_type=jnp.float32)
    second_half, degree, parity = column_terms(pair_ids)
    products = products.reshape(products.shape[0], 2, 2, 2, -1, NPAIR)
    chosen = jnp.where(second_half[:, None, None, None, :], products[:, 1], products[:, 0])
    return chosen[:, 0] + parity[:, None, None, :] * chosen[:, 1]


def helmholtz_solve(spectral_total, pair_ids, helm_coeff):
    second_half, degree, parity = column_terms(pair_ids)
    growth = (degree * (degree + 1)).astype(jnp.float32)
    return spectral_total / (1.0 + helm_coeff[None, None, :, None] * growth[:, None, None, :])


def synthesise(legend, solved, pair_ids):
    second_half, degree, parity = column_terms(pair_ids)
    rounded = solved.astype(jnp.bfloat16)
    lower_mask = jnp.where(second_half, 0.0, 1.0)
    upper_mask = jnp.where(second_half, 1.0, 0.0)
    selector = jnp.stack([lower_mask, upper_mask], axis=1)
    sign_rows = jnp.stack([jnp.ones_like(parity), parity], axis=1)
    weights = (selector[:, :, None, :] * sign_rows[:, None, :, :]).astype(jnp.bfloat16)
    spread = weights[:, :, :, None, None, :] * rounded[:, None, None, :, :, :]
    out_shape = spread.shape[:5]
    spread = spread.reshape(spread.shape[0], -1, NPAIR)
    rows_out = jnp.einsum("ksc,sqc->sqk", legend, spread, preferred_element_type=jnp.float32)
    rows_out = (4.0 * rows_out).astype(jnp.bfloat16)
    return rows_out.reshape(out_shape + (legend.shape[0],))


def on_device(grid_field, row_shift, col_shift, lon_weight, pair_of_slot, legendre, helm_coeff):
    lat_pos = lax.axis_index("lat")
    lon_pos = lax.axis_index("lon")
    lat_count = lax.axis_size("lat")
    lon_count = lax.axis_size("lon")
    band_rows = grid_field.shape[2]
    sector_cols = grid_field.shape[3]
    half_rows = band_rows * lat_count
    row_count = band_rows // lon_count
    first_row = lat_pos * band_rows + lon_pos * row_count
    widened = extended_2(grid_field, (("lon", 3),), WL)
    extended = extended_2(widened, (("lat", 2),), H)
    mirrored = widened[:, ::-1, band_rows - H :, :][:, :, ::-1, :]
    at_equator = lat_pos == lat_count - 1
    upper_rows = jnp.where(at_equator, mirrored, extended[:, :, band_rows + H :, :])
    extended = jnp.concatenate([extended[:, :, : band_rows + H, :], upper_rows], axis=2)
    advected = depart_values(
        extended,
        half_rows,
        H,
        lat_pos * band_rows,
        lon_pos * sector_cols,
        lon_pos * sector_cols - WL,
        row_shift,
        col_shift,
        lon_weight,
    )
    advected, pair_tie = lax.optimization_barrier((advected, pair_of_slot))
    row_data = lax.all_to_all(advected, "lon", split_axis=2, concat_axis=3, tiled=True)
    lat_rows = first_row + jnp.arange(row_count, dtype=jnp.int32)
    per_row = jnp.moveaxis(row_data, 2, 0)
    spectra = jax.vmap(lambda row, lat: row_spectrum(row, lat, pair_tie))(per_row, lat_rows)
    gathered = jax.tree.map(
        lambda part, own: part.astype(own.dtype),
        lax.all_to_all(shortened(spectra), "lon", split_axis=1, concat_axis=0, tiled=True),
        spectra,
    )
    slot_count = legendre.shape[1]
    pair_ids = lax.dynamic_slice_in_dim(pair_of_slot, lon_pos * slot_count, slot_count)
    partial_sum = analyse(legendre, gathered, pair_ids)
    spectral_total = lat_sum(partial_sum)
    spectral_solution = helmholtz_solve(spectral_total, pair_ids, helm_coeff)
    fourier_rows = synthesise(legendre, spectral_solution, pair_ids)
    return (spectral_solution, fourier_rows)


def solution(mesh):
    return jax.shard_map(
        on_device,
        mesh=mesh,
        in_specs=(
            P(None, None, "lat", "lon"),
            P(None, "lat", "lon"),
            P(None, "lat", "lon"),
            P(None, "lat", "lon"),
            P(),
            P("lat", "lon", None),
            P(),
        ),
        out_specs=(P("lon", None, None, None), P("lon", None, None, None, None, "lat")),
        check_vma=False,
    )
```

```python
import math

import jax
import jax.numpy as jnp
from jax import lax
from jax.experimental import pallas as pl
from jax.sharding import PartitionSpec as P

TRUNC = 1279
H = 1
PAIRS = 640
NPAIR = 1281
WL = 10


def extended_2(value, sides, width):
    for axis, dim in sides:
        peers, length = (lax.axis_size(axis), value.shape[dim])
        up = [(i, (i + 1) % peers) for i in range(peers - 1)]
        down = [(j, i) for i, j in up]
        last = lax.slice_in_dim(value, length - width, length, axis=dim)
        initial = lax.slice_in_dim(value, 0, width, axis=dim)
        before = lax.ppermute(last, axis, up)
        after = lax.ppermute(initial, axis, down)
        value = jnp.concatenate([before, value, after], axis=dim)
    return value


def shortened(value):

    def short(part):
        return part.astype(jnp.bfloat16) if part.dtype == jnp.float32 else part

    return jax.tree.map(short, value)


def depart_kernel(ext_ref, code_ref, weight_ref, out_ref):
    code = code_ref[...]
    rows, cols = code.shape[1], code.shape[2]
    left = jnp.zeros(code.shape, jnp.float32)
    right = left
    reach = ((WL - 8, WL + 6), (WL - 5, WL + 6), (WL - 5, WL + 9))
    for dr in range(ext_ref.shape[2] - rows + 1):
        for dc in range(*reach[dr]):
            window = ext_ref[0, :, dr : dr + rows, dc : dc + cols].astype(jnp.float32)
            key = dr * 64 + dc
            left = jnp.where(code == key, window, left)
            right = jnp.where(code == key - 1, window, right)
    blend = weight_ref[...].astype(jnp.float32)
    out_ref[0] = (1.0 - blend) * left + blend * right


def depart_values(
    extended, half_rows, low_rows, first_row, col_core, col_ext, row_shift, col_shift, lon_weight
):
    row_count = row_shift.shape[1]
    col_count = row_shift.shape[2]
    height = extended.shape[2]
    ext_width = extended.shape[3]
    lat_index = first_row + jnp.arange(row_count, dtype=jnp.int32)[:, None]
    lon_index = col_core + jnp.arange(col_count, dtype=jnp.int32)[None, :]
    length = 20 + 4 * lat_index
    target = jnp.maximum(lat_index + row_shift, 0)
    mirror = jnp.where(target > half_rows - 1, 2 * half_rows - 1 - target, target)
    length_dep = 20 + 4 * mirror
    shifted = jnp.clip(lon_index + col_shift, 0, length - 1)
    column = jnp.minimum(shifted * length_dep // length, length_dep - 2)
    row_off = target - first_row + low_rows - (lat_index - first_row)
    col_off = column - col_ext - (lon_index - col_core)
    code = jnp.where(lon_index < length, row_off * 64 + col_off, -4096).astype(jnp.int32)
    field_count = extended.shape[0]
    blended = pl.pallas_call(
        depart_kernel,
        grid=(field_count,),
        in_specs=[
            pl.BlockSpec((1,) + extended.shape[1:], lambda f: (f, 0, 0, 0)),
            pl.BlockSpec(code.shape, lambda f: (0, 0, 0)),
            pl.BlockSpec(code.shape, lambda f: (0, 0, 0)),
        ],
        out_specs=pl.BlockSpec((1,) + code.shape, lambda f: (f, 0, 0, 0)),
        out_shape=jax.ShapeDtypeStruct((field_count,) + code.shape, jnp.float32),
    )(extended, code, lon_weight)
    return jnp.where(lon_index < length, blended, 0.0).astype(jnp.bfloat16)


def phase_table(orders, steps, quarter_len):
    product = orders[None] * steps[:, None, None]
    whole = jnp.floor(product.astype(jnp.float32) / quarter_len.astype(jnp.float32))
    phase_idx = product - whole.astype(jnp.int32) * quarter_len
    phase_idx = jnp.where(phase_idx < 0, phase_idx + quarter_len, phase_idx)
    phase_idx = jnp.where(phase_idx >= quarter_len, phase_idx - quarter_len, phase_idx)
    angles = phase_idx.astype(jnp.float32) * (2.0 * math.pi) / quarter_len.astype(jnp.float32)
    return jnp.cos(angles), jnp.sin(angles)


def row_spectrum(row_data, lat_index, pair_of_slot):
    length = 20 + 4 * lat_index
    quarter_len = length // 4
    quarters = row_data.reshape(row_data.shape[0], 2, -1, 4)
    slot_count = quarters.shape[2]
    inner_n = 32
    outer_n = -(-slot_count // inner_n)
    offsets = jnp.arange(4, dtype=jnp.int32)[None, None, :]
    norm_scale = 1.0 / jnp.sqrt(length.astype(jnp.float32))
    pair_orders = jnp.stack([pair_of_slot, TRUNC - pair_of_slot], axis=1)
    outer_cos, outer_sin = phase_table(
        pair_orders, jnp.arange(outer_n, dtype=jnp.int32) * inner_n, quarter_len
    )
    inner_cos, inner_sin = phase_table(pair_orders, jnp.arange(inner_n, dtype=jnp.int32), quarter_len)
    cosine = outer_cos[:, None] * inner_cos[None] - outer_sin[:, None] * inner_sin[None]
    minus_sine = -(outer_sin[:, None] * inner_cos[None] + outer_cos[:, None] * inner_sin[None])
    cosine = cosine.reshape((outer_n * inner_n,) + cosine.shape[2:])[:slot_count]
    minus_sine = minus_sine.reshape((outer_n * inner_n,) + minus_sine.shape[2:])[:slot_count]
    slots = jnp.arange(slot_count, dtype=jnp.int32)[:, None, None]
    usable = (2 * pair_orders[None] < length) & (slots < quarter_len)
    factors = jnp.stack(
        [jnp.where(usable, cosine, 0.0), jnp.where(usable, minus_sine, 0.0)], axis=-1
    ).astype(jnp.bfloat16)
    inner = jnp.einsum("aser,fhab->serfhb", factors, quarters, preferred_element_type=jnp.float32)
    twist_idx = pair_orders[:, :, None] * offsets % length
    twist = twist_idx.astype(jnp.float32) * (2.0 * math.pi) / length.astype(jnp.float32)
    twist_cos = jnp.cos(twist)[:, :, None, None, :]
    twist_sin = jnp.sin(twist)[:, :, None, None, :]
    real_part = jnp.sum(inner[:, :, 0] * twist_cos + inner[:, :, 1] * twist_sin, axis=-1)
    imag_part = jnp.sum(inner[:, :, 1] * twist_cos - inner[:, :, 0] * twist_sin, axis=-1)
    spectrum = jnp.stack([real_part, imag_part], axis=2).transpose(0, 1, 4, 2, 3)
    return (spectrum * norm_scale).astype(jnp.bfloat16).reshape(PAIRS, -1)


def lat_sum(value):
    peers = lax.axis_size("lat")
    lead = value.shape[0]
    grouped = value.reshape(lead, -1, value.shape[-1])
    groups = grouped.shape[1]
    if groups % peers == 0:
        grouped = jnp.moveaxis(grouped, 1, 0)
        pieces = lax.all_to_all(grouped.astype(jnp.bfloat16), "lat", 0, 0, tiled=True)
        pieces = pieces.astype(jnp.float32).reshape((peers, groups // peers) + grouped.shape[1:])
        reduced = jnp.sum(pieces, axis=0)
        whole = lax.all_gather(reduced, "lat", axis=0, tiled=True)
        return jnp.moveaxis(whole, 0, 1).reshape(value.shape)
    count = value.size
    pad = (-count) % (peers * 1024)
    flat = jnp.pad(value.reshape(-1), (0, pad)).reshape(peers, -1, 1024)
    pieces = lax.all_to_all(flat.astype(jnp.bfloat16), "lat", 0, 0, tiled=True)
    reduced = jnp.sum(pieces.astype(jnp.float32), axis=0, keepdims=True)
    whole = lax.all_gather(reduced, "lat", axis=0, tiled=True)
    return whole.reshape(-1)[:count].reshape(value.shape)


def column_terms(pair_ids):
    columns = jnp.arange(NPAIR, dtype=jnp.int32)[None, :]
    partner = (TRUNC - pair_ids)[:, None]
    second_half = columns > partner
    degree = jnp.where(second_half, columns - 1, pair_ids[:, None] + columns)
    offset = jnp.where(second_half, columns - 1 - partner, columns)
    parity = (1 - 2 * (offset % 2)).astype(jnp.float32)
    return (second_half, degree, parity)


def analyse(legend, spectra, pair_ids):
    products = jnp.einsum("ksc,ksq->sqc", legend, spectra, preferred_element_type=jnp.float32)
    second_half, degree, parity = column_terms(pair_ids)
    products = products.reshape(products.shape[0], 2, 2, 2, -1, NPAIR)
    chosen = jnp.where(second_half[:, None, None, None, :], products[:, 1], products[:, 0])
    return chosen[:, 0] + parity[:, None, None, :] * chosen[:, 1]


def helmholtz_solve(spectral_total, pair_ids, helm_coeff):
    second_half, degree, parity = column_terms(pair_ids)
    growth = (degree * (degree + 1)).astype(jnp.float32)
    return spectral_total / (1.0 + helm_coeff[None, None, :, None] * growth[:, None, None, :])


def synthesise(legend, solved, pair_ids):
    second_half, degree, parity = column_terms(pair_ids)
    rounded = solved.astype(jnp.bfloat16)
    lower_mask = jnp.where(second_half, 0.0, 1.0)
    upper_mask = jnp.where(second_half, 1.0, 0.0)
    selector = jnp.stack([lower_mask, upper_mask], axis=1)
    sign_rows = jnp.stack([jnp.ones_like(parity), parity], axis=1)
    weights = (selector[:, :, None, :] * sign_rows[:, None, :, :]).astype(jnp.bfloat16)
    spread = weights[:, :, :, None, None, :] * rounded[:, None, None, :, :, :]
    out_shape = spread.shape[:5]
    spread = spread.reshape(spread.shape[0], -1, NPAIR)
    rows_out = jnp.einsum("ksc,sqc->sqk", legend, spread, preferred_element_type=jnp.float32)
    rows_out = (4.0 * rows_out).astype(jnp.bfloat16)
    return rows_out.reshape(out_shape + (legend.shape[0],))


def on_device(grid_field, row_shift, col_shift, lon_weight, pair_of_slot, legendre, helm_coeff):
    lat_pos = lax.axis_index("lat")
    lon_pos = lax.axis_index("lon")
    lat_count = lax.axis_size("lat")
    lon_count = lax.axis_size("lon")
    band_rows = grid_field.shape[2]
    sector_cols = grid_field.shape[3]
    half_rows = band_rows * lat_count
    row_count = band_rows // lon_count
    first_row = lat_pos * band_rows + lon_pos * row_count
    widened = extended_2(grid_field, (("lon", 3),), WL)
    extended = extended_2(widened, (("lat", 2),), H)
    mirrored = widened[:, ::-1, band_rows - H :, :][:, :, ::-1, :]
    at_equator = lat_pos == lat_count - 1
    upper_rows = jnp.where(at_equator, mirrored, extended[:, :, band_rows + H :, :])
    extended = jnp.concatenate([extended[:, :, : band_rows + H, :], upper_rows], axis=2)
    advected = depart_values(
        extended,
        half_rows,
        H,
        lat_pos * band_rows,
        lon_pos * sector_cols,
        lon_pos * sector_cols - WL,
        row_shift,
        col_shift,
        lon_weight,
    )
    advected, pair_tie = lax.optimization_barrier((advected, pair_of_slot))
    row_data = lax.all_to_all(advected, "lon", split_axis=2, concat_axis=3, tiled=True)
    lat_rows = first_row + jnp.arange(row_count, dtype=jnp.int32)
    per_row = jnp.moveaxis(row_data, 2, 0)
    spectra = jax.vmap(lambda row, lat: row_spectrum(row, lat, pair_tie))(per_row, lat_rows)
    gathered = jax.tree.map(
        lambda part, own: part.astype(own.dtype),
        lax.all_to_all(shortened(spectra), "lon", split_axis=1, concat_axis=0, tiled=True),
        spectra,
    )
    slot_count = legendre.shape[1]
    pair_ids = lax.dynamic_slice_in_dim(pair_of_slot, lon_pos * slot_count, slot_count)
    partial_sum = analyse(legendre, gathered, pair_ids)
    spectral_total = lat_sum(partial_sum)
    spectral_solution = helmholtz_solve(spectral_total, pair_ids, helm_coeff)
    fourier_rows = synthesise(legendre, spectral_solution, pair_ids)
    return (spectral_solution, fourier_rows)


def solution(mesh):
    return jax.shard_map(
        on_device,
        mesh=mesh,
        in_specs=(
            P(None, None, "lat", "lon"),
            P(None, "lat", "lon"),
            P(None, "lat", "lon"),
            P(None, "lat", "lon"),
            P(),
            P("lat", "lon", None),
            P(),
        ),
        out_specs=(P("lon", None, None, None), P("lon", None, None, None, None, "lat")),
        check_vma=False,
    )
```
